256 devices in a mesh: row: 8 (over y, core), col: 32 (over x, z).
Axes of the slice: x: 4, y: 4, z: 8, core: 2. Of those that a mesh axis runs over, the one named last changes fastest.
Arguments:
- hidden: bfloat16 [32768, 4608], P('col', 'row'), may hold values from -6 to 6
- w_query: bfloat16 [4608, 4096], P('col', 'row'), may hold values from -0.09375 to 0.09375
- w_key: bfloat16 [4608, 2048], P('col', 'row'), may hold values from -0.09375 to 0.09375
- w_value: bfloat16 [4608, 2048], P('col', 'row'), may hold values from -0.09375 to 0.09375
- adapter_down: bfloat16 [32, 4608, 32], P('col', 'row'), may hold values from -0.09375 to 0.09375
- adapter_up_query: bfloat16 [32, 16, 4096], P('col', None, 'row'), may hold values from -1.5 to 1.5
- adapter_up_value: bfloat16 [32, 16, 2048], P('col', None, 'row'), may hold values from -1.5 to 1.5
- lengths: int32 [32, 10], P('col'), may hold values from 1 to 192, 1024 in all within a row
- request_adapter: int32 [32, 10], P('col'), may hold values from 0 to 31
- adapter_slot: int32 [32], replicated, may hold values from 0 to 31, each once
- page_table: int32 [32, 18], P('col'), may hold values from 0 to 17, each once within a row
Outputs:
- query: bfloat16 [32768, 4096], P('col', 'row')
- key_cache: bfloat16 [576, 128, 2048], P('col', None, 'row')
- value_cache: bfloat16 [576, 128, 2048], P('col', None, 'row')
The draws below stay inside these ranges and needn't reach their ends.
Inputs may be any that keep to these rules, and one draw needn't show every extreme that they name: Each row of lengths sums to 1024, and its longest request has exactly 192 tokens. `adapter_slot`: a permutation of the slots. `page_table`: each row is a permutation of the 18 local slots.
All inputs are finite; a program needn't handle non-finite values.
Results may differ from the reference program's by a relative error of at most 0.0039.
Values may be sent and summed in bfloat16 or wider, within the bound.
No kernel may reach another device: no remote copies, remote signals or barrier semaphores. Data moves between devices by JAX's collectives and lax.ppermute only.
A program may use at most 128 MiB of HBM per device.

```python
import math
import jax
import jax.numpy as jnp
import numpy as np

D = 4608
HEAD = 128
RANK = 16
PAGE = 128
MOST = 192
TOK_DEV = 1024
REQ_DEV = 10
PAGES_DEV = 18
QW = 4096
KW = 2048
ADAPTERS = 32
TOKENS = 32768
CACHE_PAGES = 576
N_COL = 32


def plant(entries, rng, least, top_value):
    longest = entries.shape.index(max(entries.shape))
    spots = []
    for shift in (0, 1):
        where = [jax.random.randint(jax.random.fold_in(rng, axis), (), 0, length) for axis, length in enumerate(entries.shape)]
        where[longest] = (where[longest] + shift) % entries.shape[longest]
        spots.append(tuple(where))
    return entries.at[spots[0]].set(least).at[spots[1]].set(top_value)


def block_scale(rng, extent, shards, smallest, top_value):
    gain = 1.0
    for dim, shards_of in shards:
        draws = jax.random.uniform(jax.random.fold_in(jax.random.fold_in(rng, 6), dim), (shards_of,), jnp.float32, smallest / len(shards), top_value / len(shards))
        gain = gain * jnp.repeat(jnp.exp(draws), extent[dim] // shards_of).reshape((-1,) + (1,) * (len(extent) - 1 - dim))
    return gain


def rank_table(number_of, lean):
    weights = [(1 << 20) // math.isqrt(rank ** lean) + 1 for rank in range(1, number_of + 1)]
    scale = 1 + sum(weights) // (1 << 30)
    return np.cumsum(np.array([max(1, weight // scale) for weight in weights]))


def ranked(own_key, extent, amount, lean):
    listing = rank_table(amount, lean)
    ticket = jax.random.randint(jax.random.fold_in(own_key, 1), extent, 0, int(listing[amount - 1]))
    grade = jnp.searchsorted(jnp.asarray(listing, jnp.int32), ticket, side="right")
    return jax.random.permutation(jax.random.fold_in(own_key, 2), amount)[grade].astype(jnp.int32)


def length_profile(amount, total, limit, lean):
    portions = [(1 << 20) // math.isqrt(grade ** lean) + 1 for grade in range(2, amount + 1)]
    spare, given = total - limit - (amount - 1), [1] * (amount - 1)
    while spare > 0:
        candidates = [i for i in range(amount - 1) if given[i] < limit]
        mass, budget = sum([portions[i] for i in candidates]), spare
        for i in candidates:
            addition = min(limit - given[i], max(1, budget * portions[i] // mass), spare)
            given[i] = given[i] + addition
            spare = spare - addition
    return np.array([limit] + given)


def ragged(key, number_of, total, bound, skew):
    if number_of == 2:
        one = jax.random.randint(key, (), max(1, total - bound), min(bound, total - 1) + 1)
        return jnp.stack([one, total - one])
    tallies = jnp.asarray(length_profile(number_of, total, bound, skew), jnp.int32)
    couples = (number_of - 1) // 2
    source_of, sink = tallies[1:1 + 2 * couples:2], tallies[2:2 + 2 * couples:2]
    slack = jnp.minimum(source_of - 1, bound - sink)
    shifted = jax.random.randint(jax.random.fold_in(key, 1), (couples,), 0, 1 << 20) % (slack + 1)
    tallies = tallies.at[1:1 + 2 * couples:2].set(source_of - shifted).at[2:2 + 2 * couples:2].set(sink + shifted)
    return tallies[jax.random.permutation(jax.random.fold_in(key, 2), number_of)]


def bell_draw(own_key, extent, spread, limit, cuts=(), held_as=jnp.bfloat16):
    factor_of = block_scale(own_key, extent, cuts, -0.22, 0.18) if cuts else 1.0
    entries = jax.random.normal(own_key, extent, jnp.float32) * spread * factor_of
    return jnp.minimum(jnp.maximum(entries, -limit), limit).astype(held_as)


def setup_inputs(seed: int = 0) -> dict:
    streams_of = jax.random.split(jax.random.key(seed), 12)
    hidden = bell_draw(streams_of[0], (TOKENS, D), 1.0, 6.0, ((0, 32), (1, 8)))
    w_query = bell_draw(streams_of[1], (D, QW), D ** -0.5, 0.09375, ((0, 32), (1, 8)))
    w_key = bell_draw(streams_of[2], (D, KW), D ** -0.5, 0.09375, ((0, 32), (1, 8)))
    w_value = bell_draw(streams_of[3], (D, KW), D ** -0.5, 0.09375, ((0, 32), (1, 8)))
    adapter_down = bell_draw(streams_of[4], (ADAPTERS, D, 2 * RANK), D ** -0.5, 0.09375, ((0, 32), (1, 8)))
    adapter_up_query = bell_draw(streams_of[5], (ADAPTERS, RANK, QW), RANK ** -0.5, 1.5, ((0, 32), (2, 8)))
    adapter_up_value = bell_draw(streams_of[6], (ADAPTERS, RANK, KW), RANK ** -0.5, 1.5, ((0, 32), (2, 8)))
    lengths = jax.vmap(lambda own: ragged(own, REQ_DEV, TOK_DEV, MOST, 2))(jax.random.split(streams_of[7], N_COL)).reshape((N_COL, REQ_DEV)).astype(jnp.int32)
    request_adapter = plant(ranked(streams_of[8], (N_COL, REQ_DEV), ADAPTERS, 2), jax.random.fold_in(streams_of[8], 3), 0, ADAPTERS - 1).astype(jnp.int32)
    adapter_slot = jax.random.permutation(streams_of[9], ADAPTERS).astype(jnp.int32)
    page_table = jax.vmap(lambda own: jax.random.permutation(own, PAGES_DEV))(jax.random.split(streams_of[10], N_COL)).reshape((N_COL, PAGES_DEV)).astype(jnp.int32)
    return dict(hidden=hidden, w_query=w_query, w_key=w_key, w_value=w_value, adapter_down=adapter_down, adapter_up_query=adapter_up_query, adapter_up_value=adapter_up_value, lengths=lengths, request_adapter=request_adapter, adapter_slot=adapter_slot, page_table=page_table)


def rotate(values, position):
    half_width = HEAD // 2
    frequency = jnp.exp(jnp.arange(half_width, dtype=jnp.float32) * (-2.0 * math.log(10000.0) / HEAD))
    angles = position.astype(jnp.float32)[:, None] * frequency[None, :]
    cosine = jnp.cos(angles)[:, None, :]
    sine_value = jnp.sin(angles)[:, None, :]
    shaped = values.reshape(values.shape[0], -1, HEAD)
    leading = shaped[:, :, :half_width]
    second = shaped[:, :, half_width:]
    rotated = jnp.concatenate([leading * cosine - second * sine_value, second * cosine + leading * sine_value], axis=2)
    return rotated.reshape(values.shape)


def layout(lengths, page_row):
    token_index = jnp.arange(TOK_DEV, dtype=jnp.int32)
    starts = (jnp.cumsum(lengths) - lengths).astype(jnp.int32)
    request_of = (jnp.sum((token_index[:, None] >= starts[None, :]).astype(jnp.int32), axis=1) - 1).astype(jnp.int32)
    position = (token_index - jnp.take(starts, request_of)).astype(jnp.int32)
    pages_each = ((lengths + PAGE - 1) // PAGE).astype(jnp.int32)
    page_start = (jnp.cumsum(pages_each) - pages_each).astype(jnp.int32)
    page_index = (jnp.take(page_start, request_of) + position // PAGE).astype(jnp.int32)
    target = (jnp.take(page_row, page_index) * PAGE + position % PAGE).astype(jnp.int32)
    return starts, request_of, position, target


def expand_up(lowrank, chosen, up_query, up_value):
    adapter_count = up_query.shape[0]
    rank_width = up_query.shape[1]
    onehot = (chosen[:, None] == jnp.arange(adapter_count, dtype=jnp.int32)[None, :]).astype(lowrank.dtype)
    spread_query = (onehot[:, :, None] * lowrank[:, None, :rank_width]).reshape(-1, adapter_count * rank_width)
    spread_value = (onehot[:, :, None] * lowrank[:, None, rank_width:]).reshape(-1, adapter_count * rank_width)
    delta_query = jnp.dot(spread_query, up_query.reshape(adapter_count * rank_width, -1), preferred_element_type=jnp.float32)
    delta_value = jnp.dot(spread_value, up_value.reshape(adapter_count * rank_width, -1), preferred_element_type=jnp.float32)
    return delta_query, delta_value


def reference(hidden, w_query, w_key, w_value, adapter_down, adapter_up_query, adapter_up_value, lengths, request_adapter, adapter_slot, page_table):
    starts, request_of, position, target = jax.vmap(layout)(lengths, page_table)
    offsets = (jnp.arange(N_COL, dtype=jnp.int32) * (PAGES_DEV * PAGE))[:, None]
    target = (target + offsets).reshape(-1)
    position = position.reshape(-1)
    chosen = jnp.take(adapter_slot, jnp.take_along_axis(request_adapter, request_of, axis=1)).reshape(-1)
    base_query = jnp.dot(hidden, w_query, preferred_element_type=jnp.float32)
    base_key = jnp.dot(hidden, w_key, preferred_element_type=jnp.float32)
    base_value = jnp.dot(hidden, w_value, preferred_element_type=jnp.float32)
    stacked_down = jnp.transpose(adapter_down, (1, 0, 2)).reshape(D, ADAPTERS * 2 * RANK)
    lowrank_all = jnp.dot(hidden, stacked_down, preferred_element_type=jnp.float32).reshape(-1, ADAPTERS, 2 * RANK)
    lowrank = jnp.take_along_axis(lowrank_all, chosen[:, None, None], axis=1)[:, 0].astype(jnp.bfloat16)
    delta_query, delta_value = expand_up(lowrank, chosen, adapter_up_query, adapter_up_value)
    query = rotate(base_query + delta_query, position).astype(jnp.bfloat16)
    key_rotated = rotate(base_key, position).astype(jnp.bfloat16)
    value_rows = (base_value + delta_value).astype(jnp.bfloat16)
    key_cache = jnp.zeros((CACHE_PAGES * PAGE, KW), jnp.bfloat16).at[target].set(key_rotated).reshape(CACHE_PAGES, PAGE, KW)
    value_cache = jnp.zeros((CACHE_PAGES * PAGE, KW), jnp.bfloat16).at[target].set(value_rows).reshape(CACHE_PAGES, PAGE, KW)
    return (query, key_cache, value_cache)
```

```python
import math

import jax
import jax.numpy as jnp
from jax import lax
from jax.sharding import PartitionSpec as P

HEAD = 128
PAGE = 128
TOK_DEV = 1024


def rotate(values, cosine, sine_value):
    half_width = HEAD // 2
    shaped = values.reshape(values.shape[0], -1, HEAD)
    leading = shaped[:, :, :half_width]
    second = shaped[:, :, half_width:]
    rotated = jnp.concatenate(
        [leading * cosine - second * sine_value, second * cosine + leading * sine_value], axis=2
    )
    return rotated.reshape(values.shape)


def token_layout(lengths, chosen_request):
    token_index = jnp.arange(TOK_DEV, dtype=jnp.int32)
    starts = jnp.cumsum(lengths) - lengths
    inside = (token_index[:, None] >= starts[None, :]) & (
        token_index[:, None] < (starts + lengths)[None, :]
    )
    inside = inside.astype(jnp.int32)
    position = token_index - jnp.sum(inside * starts[None, :], axis=1)
    chosen = jnp.sum(inside * chosen_request[None, :], axis=1)
    return starts, position, chosen


def cache_rows(lengths, starts, page_row):
    pages = page_row.shape[0]
    pages_each = (lengths + PAGE - 1) // PAGE
    page_start = jnp.cumsum(pages_each) - pages_each
    page_ids = jnp.arange(pages, dtype=jnp.int32)
    owner = (page_row[:, None] == page_ids[None, :]).astype(jnp.int32)
    page_of_slot = jnp.sum(owner * page_ids[:, None], axis=0)
    member = (page_of_slot[:, None] >= page_start[None, :]) & (
        page_of_slot[:, None] < (page_start + pages_each)[None, :]
    )
    member = member.astype(jnp.int32)
    used = jnp.sum(member, axis=1) > 0
    first_page = jnp.sum(member * page_start[None, :], axis=1)
    first_token = jnp.sum(member * starts[None, :], axis=1)
    length = jnp.sum(member * lengths[None, :], axis=1)
    offset = (page_of_slot - first_page) * PAGE
    source = first_token + offset
    valid = jnp.where(used, jnp.minimum(length - offset, PAGE), 0)
    inner = jnp.arange(PAGE, dtype=jnp.int32)
    rows = (source[:, None] + inner[None, :]).reshape(-1)
    keep = (inner[None, :] < valid[:, None]).reshape(-1)
    rows = jnp.clip(rows, 0, TOK_DEV - 1)
    return rows, keep


def shards(
    hidden,
    w_query,
    w_key,
    w_value,
    adapter_down,
    adapter_up_query,
    adapter_up_value,
    lengths,
    request_adapter,
    adapter_slot,
    page_table,
):
    lengths = lengths[0]
    chosen_request = jnp.take(adapter_slot, request_adapter[0])
    starts, position, chosen = token_layout(lengths, chosen_request)
    adapter_count = adapter_slot.shape[0]
    rank_width = adapter_up_query.shape[1]
    query_width = w_query.shape[1]
    key_width = w_key.shape[1]

    weight_width = query_width + 2 * key_width
    feature_rows = w_query.shape[0]
    down_shape = adapter_down.shape[1:]
    row_size = lax.axis_size("row")

    with jax.named_scope("gathers"):
        full_rows = lax.all_gather(hidden, "row", axis=1, tiled=True)
        pieces = [
            jnp.concatenate([w_query, w_key, w_value], axis=1),
            adapter_down.reshape(-1, weight_width),
            adapter_up_query.reshape(-1, weight_width),
            adapter_up_value.reshape(-1, weight_width),
        ]
        bounds = [0]
        for piece in pieces:
            bounds.append(bounds[-1] + piece.shape[0])
        packed = lax.all_gather(jnp.concatenate(pieces, axis=0), "col", axis=0)
        weights = packed[:, : bounds[1]].reshape(-1, weight_width)
        down_local = packed[:, bounds[1] : bounds[2]].reshape((adapter_count,) + down_shape)
        up_query = packed[:, bounds[2] : bounds[3]].reshape(adapter_count, rank_width, -1)
        up_value = packed[:, bounds[3] : bounds[4]].reshape(adapter_count, rank_width, -1)

    with jax.named_scope("lowrank"):
        onehot = (chosen[:, None] == jnp.arange(adapter_count, dtype=jnp.int32)[None, :])
        partial_all = jnp.einsum(
            "tf,sfr->tsr", hidden, down_local, preferred_element_type=jnp.float32
        )
        partial = jnp.sum(jnp.where(onehot[:, :, None], partial_all, 0.0), axis=1)
        distance = 1
        while distance < row_size:
            pairs = [(i, i ^ distance) for i in range(row_size)]
            partial = partial + lax.ppermute(partial, "row", pairs)
            distance *= 2
        lowrank = partial.astype(jnp.bfloat16)
        onehot_b = onehot.astype(jnp.bfloat16)
        spread_query = (onehot_b[:, :, None] * lowrank[:, None, :rank_width]).reshape(
            -1, adapter_count * rank_width
        )
        spread_value = (onehot_b[:, :, None] * lowrank[:, None, rank_width:]).reshape(
            -1, adapter_count * rank_width
        )
        delta_query = jnp.dot(
            spread_query,
            up_query.reshape(adapter_count * rank_width, -1),
            preferred_element_type=jnp.float32,
        )
        delta_value = jnp.dot(
            spread_value,
            up_value.reshape(adapter_count * rank_width, -1),
            preferred_element_type=jnp.float32,
        )

    with jax.named_scope("projection"):
        base = jnp.dot(full_rows, weights, preferred_element_type=jnp.float32)
        base_query = base[:, :query_width]
        base_key = base[:, query_width : query_width + key_width]
        base_value = base[:, query_width + key_width :]

    with jax.named_scope("rotary"):
        half_width = HEAD // 2
        frequency = jnp.exp(
            jnp.arange(half_width, dtype=jnp.float32) * (-2.0 * math.log(10000.0) / HEAD)
        )
        angles = position.astype(jnp.float32)[:, None] * frequency[None, :]
        cosine = jnp.cos(angles)[:, None, :]
        sine_value = jnp.sin(angles)[:, None, :]
        query = rotate(base_query + delta_query, cosine, sine_value).astype(jnp.bfloat16)
        key_rotated = rotate(base_key, cosine, sine_value).astype(jnp.bfloat16)
        value_rows = (base_value + delta_value).astype(jnp.bfloat16)

    with jax.named_scope("cache_write"):
        pages = page_table.shape[1]
        rows, keep = cache_rows(lengths, starts, page_table[0])
        key_cache = jnp.where(keep[:, None], jnp.take(key_rotated, rows, axis=0), 0).reshape(
            pages, PAGE, key_width
        )
        value_cache = jnp.where(keep[:, None], jnp.take(value_rows, rows, axis=0), 0).reshape(
            pages, PAGE, key_width
        )
    return (query, key_cache.astype(jnp.bfloat16), value_cache.astype(jnp.bfloat16))


def solution(mesh):
    return jax.shard_map(
        shards,
        mesh=mesh,
        in_specs=(
            P("col", "row"),
            P("col", "row"),
            P("col", "row"),
            P("col", "row"),
            P("col", "row", None),
            P("col", None, "row"),
            P("col", None, "row"),
            P("col", None),
            P("col", None),
            P(),
            P("col", None),
        ),
        out_specs=(P("col", "row"), P("col", None, "row"), P("col", None, "row")),
        check_vma=False,
    )
```

```python
import math

import jax
import jax.numpy as jnp
from jax import lax
from jax.sharding import PartitionSpec as P

HEAD = 128
PAGE = 128
TOK_DEV = 1024


def rotate(values, cosine, sine_value):
    half_width = HEAD // 2
    shaped = values.reshape(values.shape[0], -1, HEAD)
    leading = shaped[:, :, :half_width]
    second = shaped[:, :, half_width:]
    rotated = jnp.concatenate(
        [leading * cosine - second * sine_value, second * cosine + leading * sine_value], axis=2
    )
    return rotated.reshape(values.shape)


def token_layout(lengths, chosen_request):
    token_index = jnp.arange(TOK_DEV, dtype=jnp.int32)
    starts = jnp.cumsum(lengths) - lengths
    inside = (token_index[:, None] >= starts[None, :]) & (
        token_index[:, None] < (starts + lengths)[None, :]
    )
    inside = inside.astype(jnp.int32)
    position = token_index - jnp.sum(inside * starts[None, :], axis=1)
    chosen = jnp.sum(inside * chosen_request[None, :], axis=1)
    return starts, position, chosen


def cache_rows(lengths, starts, page_row):
    pages = page_row.shape[0]
    pages_each = (lengths + PAGE - 1) // PAGE
    page_start = jnp.cumsum(pages_each) - pages_each
    page_ids = jnp.arange(pages, dtype=jnp.int32)
    owner = (page_row[:, None] == page_ids[None, :]).astype(jnp.int32)
    page_of_slot = jnp.sum(owner * page_ids[:, None], axis=0)
    member = (page_of_slot[:, None] >= page_start[None, :]) & (
        page_of_slot[:, None] < (page_start + pages_each)[None, :]
    )
    member = member.astype(jnp.int32)
    used = jnp.sum(member, axis=1) > 0
    first_page = jnp.sum(member * page_start[None, :], axis=1)
    first_token = jnp.sum(member * starts[None, :], axis=1)
    length = jnp.sum(member * lengths[None, :], axis=1)
    offset = (page_of_slot - first_page) * PAGE
    source = first_token + offset
    valid = jnp.where(used, jnp.minimum(length - offset, PAGE), 0)
    inner = jnp.arange(PAGE, dtype=jnp.int32)
    rows = (source[:, None] + inner[None, :]).reshape(-1)
    keep = (inner[None, :] < valid[:, None]).reshape(-1)
    rows = jnp.clip(rows, 0, TOK_DEV - 1)
    return rows, keep


def gather_rows(hidden, row_size):
    chips = row_size // 2
    assert chips == 4
    tokens, width = hidden.shape
    index = lax.axis_index("row")
    core = index % 2
    chip = index // 2
    step = 2 * core - 1
    swap = [(i, i ^ 1) for i in range(row_size)]
    ring = [
        (i, ((i // 2 + 1) % chips) * 2 if i % 2 == 0 else ((i // 2 - 1) % chips) * 2 + 1)
        for i in range(row_size)
    ]
    partner = lax.ppermute(hidden, "row", swap)
    own_block = jnp.where(
        core == 0,
        jnp.concatenate([hidden, partner], axis=1),
        jnp.concatenate([partner, hidden], axis=1),
    )
    near = lax.ppermute(own_block, "row", ring)
    half = tokens // 2
    forwarded = lax.dynamic_slice_in_dim(near, core * half, half, 0)
    far_half = lax.ppermute(forwarded, "row", ring)
    from_partner, far_other = lax.ppermute((near, far_half), "row", swap)
    block = 2 * width
    full = jnp.zeros((tokens, chips * block), hidden.dtype)
    full = lax.dynamic_update_slice(full, own_block, (0, chip * block))
    full = lax.dynamic_update_slice(full, near, (0, ((chip + step) % chips) * block))
    full = lax.dynamic_update_slice(full, from_partner, (0, ((chip - step) % chips) * block))
    far = ((chip + 2) % chips) * block
    full = lax.dynamic_update_slice(full, far_half, (core * half, far))
    full = lax.dynamic_update_slice(full, far_other, ((1 - core) * half, far))
    return full


def shards(
    hidden,
    w_query,
    w_key,
    w_value,
    adapter_down,
    adapter_up_query,
    adapter_up_value,
    lengths,
    request_adapter,
    adapter_slot,
    page_table,
):
    lengths = lengths[0]
    chosen_request = jnp.take(adapter_slot, request_adapter[0])
    starts, position, chosen = token_layout(lengths, chosen_request)
    adapter_count = adapter_slot.shape[0]
    rank_width = adapter_up_query.shape[1]
    query_width = w_query.shape[1]
    key_width = w_key.shape[1]

    weight_width = query_width + 2 * key_width
    feature_rows = w_query.shape[0]
    down_shape = adapter_down.shape[1:]
    row_size = lax.axis_size("row")

    with jax.named_scope("gathers"):
        full_rows = gather_rows(hidden, row_size)
        pieces = [
            jnp.concatenate([w_query, w_key, w_value], axis=1),
            adapter_down.reshape(-1, weight_width),
            adapter_up_query.reshape(-1, weight_width),
            adapter_up_value.reshape(-1, weight_width),
        ]
        bounds = [0]
        for piece in pieces:
            bounds.append(bounds[-1] + piece.shape[0])
        packed = lax.all_gather(jnp.concatenate(pieces, axis=0), "col", axis=0)
        weights = packed[:, : bounds[1]].reshape(-1, weight_width)
        down_local = packed[:, bounds[1] : bounds[2]].reshape((adapter_count,) + down_shape)
        up_query = packed[:, bounds[2] : bounds[3]].reshape(adapter_count, rank_width, -1)
        up_value = packed[:, bounds[3] : bounds[4]].reshape(adapter_count, rank_width, -1)

    with jax.named_scope("lowrank"):
        onehot = (chosen[:, None] == jnp.arange(adapter_count, dtype=jnp.int32)[None, :])
        partial_all = jnp.einsum(
            "tf,sfr->tsr", hidden, down_local, preferred_element_type=jnp.float32
        )
        partial = jnp.sum(jnp.where(onehot[:, :, None], partial_all, 0.0), axis=1)
        distance = 1
        while distance < row_size:
            pairs = [(i, i ^ distance) for i in range(row_size)]
            partial = partial + lax.ppermute(partial, "row", pairs)
            distance *= 2
        lowrank = partial.astype(jnp.bfloat16)
        onehot_b = onehot.astype(jnp.bfloat16)
        spread_query = (onehot_b[:, :, None] * lowrank[:, None, :rank_width]).reshape(
            -1, adapter_count * rank_width
        )
        spread_value = (onehot_b[:, :, None] * lowrank[:, None, rank_width:]).reshape(
            -1, adapter_count * rank_width
        )
        delta_query = jnp.dot(
            spread_query,
            up_query.reshape(adapter_count * rank_width, -1),
            preferred_element_type=jnp.float32,
        )
        delta_value = jnp.dot(
            spread_value,
            up_value.reshape(adapter_count * rank_width, -1),
            preferred_element_type=jnp.float32,
        )

    with jax.named_scope("projection"):
        base = jnp.dot(full_rows, weights, preferred_element_type=jnp.float32)
        base_query = base[:, :query_width]
        base_key = base[:, query_width : query_width + key_width]
        base_value = base[:, query_width + key_width :]

    with jax.named_scope("rotary"):
        half_width = HEAD // 2
        frequency = jnp.exp(
            jnp.arange(half_width, dtype=jnp.float32) * (-2.0 * math.log(10000.0) / HEAD)
        )
        angles = position.astype(jnp.float32)[:, None] * frequency[None, :]
        cosine = jnp.cos(angles)[:, None, :]
        sine_value = jnp.sin(angles)[:, None, :]
        query = rotate(base_query + delta_query, cosine, sine_value).astype(jnp.bfloat16)
        key_rotated = rotate(base_key, cosine, sine_value).astype(jnp.bfloat16)
        value_rows = (base_value + delta_value).astype(jnp.bfloat16)

    with jax.named_scope("cache_write"):
        pages = page_table.shape[1]
        rows, keep = cache_rows(lengths, starts, page_table[0])
        select = (
            (rows[:, None] == jnp.arange(TOK_DEV, dtype=jnp.int32)[None, :]) & keep[:, None]
        ).astype(jnp.bfloat16)
        both = jnp.dot(
            select,
            jnp.concatenate([key_rotated, value_rows], axis=1),
            preferred_element_type=jnp.float32,
        ).astype(jnp.bfloat16)
        key_cache = both[:, :key_width].reshape(pages, PAGE, key_width)
        value_cache = both[:, key_width:].reshape(pages, PAGE, key_width)
    return (query, key_cache.astype(jnp.bfloat16), value_cache.astype(jnp.bfloat16))


def solution(mesh):
    return jax.shard_map(
        shards,
        mesh=mesh,
        in_specs=(
            P("col", "row"),
            P("col", "row"),
            P("col", "row"),
            P("col", "row"),
            P("col", "row", None),
            P("col", None, "row"),
            P("col", None, "row"),
            P("col", None),
            P("col", None),
            P(),
            P("col", None),
        ),
        out_specs=(P("col", "row"), P("col", None, "row"), P("col", None, "row")),
        check_vma=False,
    )
```

```python
import math

import jax
import jax.numpy as jnp
from jax import lax
from jax.sharding import PartitionSpec as P

HEAD = 128
PAGE = 128
TOK_DEV = 1024


def rotate(values, cosine, sine_value):
    half_width = HEAD // 2
    shaped = values.reshape(values.shape[0], -1, HEAD)
    leading = shaped[:, :, :half_width]
    second = shaped[:, :, half_width:]
    rotated = jnp.concatenate(
        [leading * cosine - second * sine_value, second * cosine + leading * sine_value], axis=2
    )
    return rotated.reshape(values.shape)


def token_layout(lengths, chosen_request):
    token_index = jnp.arange(TOK_DEV, dtype=jnp.int32)
    starts = jnp.cumsum(lengths) - lengths
    inside = (token_index[:, None] >= starts[None, :]) & (
        token_index[:, None] < (starts + lengths)[None, :]
    )
    inside = inside.astype(jnp.int32)
    position = token_index - jnp.sum(inside * starts[None, :], axis=1)
    chosen = jnp.sum(inside * chosen_request[None, :], axis=1)
    return starts, position, chosen


def cache_rows(lengths, starts, page_row):
    pages = page_row.shape[0]
    pages_each = (lengths + PAGE - 1) // PAGE
    page_start = jnp.cumsum(pages_each) - pages_each
    page_ids = jnp.arange(pages, dtype=jnp.int32)
    owner = (page_row[:, None] == page_ids[None, :]).astype(jnp.int32)
    page_of_slot = jnp.sum(owner * page_ids[:, None], axis=0)
    member = (page_of_slot[:, None] >= page_start[None, :]) & (
        page_of_slot[:, None] < (page_start + pages_each)[None, :]
    )
    member = member.astype(jnp.int32)
    used = jnp.sum(member, axis=1) > 0
    first_page = jnp.sum(member * page_start[None, :], axis=1)
    first_token = jnp.sum(member * starts[None, :], axis=1)
    length = jnp.sum(member * lengths[None, :], axis=1)
    offset = (page_of_slot - first_page) * PAGE
    source = first_token + offset
    valid = jnp.where(used, jnp.minimum(length - offset, PAGE), 0)
    inner = jnp.arange(PAGE, dtype=jnp.int32)
    rows = (source[:, None] + inner[None, :]).reshape(-1)
    keep = (inner[None, :] < valid[:, None]).reshape(-1)
    rows = jnp.clip(rows, 0, TOK_DEV - 1)
    return rows, keep


def gather_rows(hidden, row_size):
    chips = row_size // 2
    assert chips == 4
    tokens, width = hidden.shape
    index = lax.axis_index("row")
    core = index % 2
    chip = index // 2
    step = 2 * core - 1
    swap = [(i, i ^ 1) for i in range(row_size)]
    ring = [
        (i, ((i // 2 + 1) % chips) * 2 if i % 2 == 0 else ((i // 2 - 1) % chips) * 2 + 1)
        for i in range(row_size)
    ]
    partner = lax.ppermute(hidden, "row", swap)
    own_block = jnp.where(
        core == 0,
        jnp.concatenate([hidden, partner], axis=1),
        jnp.concatenate([partner, hidden], axis=1),
    )
    near = lax.ppermute(own_block, "row", ring)
    half = tokens // 2
    forwarded = lax.dynamic_slice_in_dim(near, core * half, half, 0)
    far_half = lax.ppermute(forwarded, "row", ring)
    from_partner, far_other = lax.ppermute((near, far_half), "row", swap)
    first = core == 0
    after = jnp.where(first, from_partner, near)
    before = jnp.where(first, near, from_partner)
    far = jnp.where(
        first,
        jnp.concatenate([far_half, far_other], axis=0),
        jnp.concatenate([far_other, far_half], axis=0),
    )
    blocks = []
    for k in range(chips):
        relative = (k - chip) % chips
        blocks.append(
            jnp.where(
                relative == 0,
                own_block,
                jnp.where(relative == 1, after, jnp.where(relative == 2, far, before)),
            )
        )
    full = jnp.concatenate(blocks, axis=1)
    return full


def shards(
    hidden,
    w_query,
    w_key,
    w_value,
    adapter_down,
    adapter_up_query,
    adapter_up_value,
    lengths,
    request_adapter,
    adapter_slot,
    page_table,
):
    lengths = lengths[0]
    chosen_request = jnp.take(adapter_slot, request_adapter[0])
    starts, position, chosen = token_layout(lengths, chosen_request)
    adapter_count = adapter_slot.shape[0]
    rank_width = adapter_up_query.shape[1]
    query_width = w_query.shape[1]
    key_width = w_key.shape[1]

    weight_width = query_width + 2 * key_width
    feature_rows = w_query.shape[0]
    down_shape = adapter_down.shape[1:]
    row_size = lax.axis_size("row")

    with jax.named_scope("gathers"):
        full_rows = gather_rows(hidden, row_size)
        features = down_shape[0]
        down_rows = jnp.pad(
            jnp.transpose(adapter_down[0]), ((0, 0), (0, weight_width - features))
        )
        pieces = [
            jnp.concatenate([w_query, w_key, w_value], axis=1),
            down_rows,
            adapter_up_query.reshape(-1, weight_width),
            adapter_up_value.reshape(-1, weight_width),
        ]
        pieces = [jnp.pad(p, ((0, -p.shape[0] % 8), (0, 0))) for p in pieces]
        bounds = [0]
        for piece in pieces:
            bounds.append(bounds[-1] + piece.shape[0])
        packed = lax.all_gather(jnp.concatenate(pieces, axis=0), "col", axis=0)
        weights = packed[:, :feature_rows]
        down_local = packed[:, bounds[1] : bounds[2]].reshape(-1, weight_width)
        up_query = packed[:, bounds[2] : bounds[3]].reshape(adapter_count, -1)
        up_query = up_query[:, : rank_width * query_width].reshape(adapter_count, rank_width, -1)
        up_value = packed[:, bounds[3] : bounds[4]].reshape(adapter_count, -1)
        up_value = up_value[:, : rank_width * key_width].reshape(adapter_count, rank_width, -1)

    with jax.named_scope("lowrank"):
        onehot = (chosen[:, None] == jnp.arange(adapter_count, dtype=jnp.int32)[None, :])
        padded_hidden = jnp.pad(hidden, ((0, 0), (0, weight_width - features)))
        partial_all = lax.dot_general(
            padded_hidden,
            down_local,
            (((1,), (1,)), ((), ())),
            preferred_element_type=jnp.float32,
        ).reshape(hidden.shape[0], adapter_count, -1)
        partial = jnp.sum(jnp.where(onehot[:, :, None], partial_all, 0.0), axis=1)
        distance = 1
        while distance < row_size:
            pairs = [(i, i ^ distance) for i in range(row_size)]
            partial = partial + lax.ppermute(partial, "row", pairs)
            distance *= 2
        lowrank = partial.astype(jnp.bfloat16)
        onehot_b = onehot.astype(jnp.bfloat16)
        spread_query = (onehot_b[:, :, None] * lowrank[:, None, :rank_width]).reshape(
            -1, adapter_count * rank_width
        )
        spread_value = (onehot_b[:, :, None] * lowrank[:, None, rank_width:]).reshape(
            -1, adapter_count * rank_width
        )
        delta_query = jnp.dot(
            spread_query,
            up_query.reshape(adapter_count * rank_width, -1),
            preferred_element_type=jnp.float32,
        )
        delta_value = jnp.dot(
            spread_value,
            up_value.reshape(adapter_count * rank_width, -1),
            preferred_element_type=jnp.float32,
        )

    with jax.named_scope("projection"):
        base = jnp.einsum(
            "tci,cin->tn",
            full_rows.reshape(full_rows.shape[0], packed.shape[0], feature_rows),
            weights,
            preferred_element_type=jnp.float32,
        )
        base_query = base[:, :query_width]
        base_key = base[:, query_width : query_width + key_width]
        base_value = base[:, query_width + key_width :]

    with jax.named_scope("rotary"):
        half_width = HEAD // 2
        frequency = jnp.exp(
            jnp.arange(half_width, dtype=jnp.float32) * (-2.0 * math.log(10000.0) / HEAD)
        )
        angles = position.astype(jnp.float32)[:, None] * frequency[None, :]
        cosine = jnp.cos(angles)[:, None, :]
        sine_value = jnp.sin(angles)[:, None, :]
        query = rotate(base_query + delta_query, cosine, sine_value).astype(jnp.bfloat16)
        key_rotated = rotate(base_key, cosine, sine_value).astype(jnp.bfloat16)
        value_rows = (base_value + delta_value).astype(jnp.bfloat16)

    with jax.named_scope("cache_write"):
        pages = page_table.shape[1]
        rows, keep = cache_rows(lengths, starts, page_table[0])
        select = (
            (rows[:, None] == jnp.arange(TOK_DEV, dtype=jnp.int32)[None, :]) & keep[:, None]
        ).astype(jnp.bfloat16)
        both = jnp.dot(
            select,
            jnp.concatenate([key_rotated, value_rows], axis=1),
            preferred_element_type=jnp.float32,
        ).astype(jnp.bfloat16)
        key_cache = both[:, :key_width].reshape(pages, PAGE, key_width)
        value_cache = both[:, key_width:].reshape(pages, PAGE, key_width)
    return (query, key_cache.astype(jnp.bfloat16), value_cache.astype(jnp.bfloat16))


def solution(mesh):
    return jax.shard_map(
        shards,
        mesh=mesh,
        in_specs=(
            P("col", "row"),
            P("col", "row"),
            P("col", "row"),
            P("col", "row"),
            P("col", "row", None),
            P("col", None, "row"),
            P("col", None, "row"),
            P("col", None),
            P("col", None),
            P(),
            P("col", None),
        ),
        out_specs=(P("col", "row"), P("col", None, "row"), P("col", None, "row")),
        check_vma=False,
    )
```

```python
import math

import jax
import jax.numpy as jnp
from jax import lax
from jax.sharding import PartitionSpec as P

HEAD = 128
PAGE = 128
TOK_DEV = 1024


def rotate(values, cosine, sine_value):
    half_width = HEAD // 2
    shaped = values.reshape(values.shape[0], -1, HEAD)
    leading = shaped[:, :, :half_width]
    second = shaped[:, :, half_width:]
    rotated = jnp.concatenate(
        [leading * cosine - second * sine_value, second * cosine + leading * sine_value], axis=2
    )
    return rotated.reshape(values.shape)


def token_layout(lengths, chosen_request):
    token_index = jnp.arange(TOK_DEV, dtype=jnp.int32)
    starts = jnp.cumsum(lengths) - lengths
    inside = (token_index[:, None] >= starts[None, :]) & (
        token_index[:, None] < (starts + lengths)[None, :]
    )
    inside = inside.astype(jnp.int32)
    position = token_index - jnp.sum(inside * starts[None, :], axis=1)
    chosen = jnp.sum(inside * chosen_request[None, :], axis=1)
    return starts, position, chosen


def cache_rows(lengths, starts, page_row):
    pages = page_row.shape[0]
    pages_each = (lengths + PAGE - 1) // PAGE
    page_start = jnp.cumsum(pages_each) - pages_each
    page_ids = jnp.arange(pages, dtype=jnp.int32)
    owner = (page_row[:, None] == page_ids[None, :]).astype(jnp.int32)
    page_of_slot = jnp.sum(owner * page_ids[:, None], axis=0)
    member = (page_of_slot[:, None] >= page_start[None, :]) & (
        page_of_slot[:, None] < (page_start + pages_each)[None, :]
    )
    member = member.astype(jnp.int32)
    used = jnp.sum(member, axis=1) > 0
    first_page = jnp.sum(member * page_start[None, :], axis=1)
    first_token = jnp.sum(member * starts[None, :], axis=1)
    length = jnp.sum(member * lengths[None, :], axis=1)
    offset = (page_of_slot - first_page) * PAGE
    source = first_token + offset
    valid = jnp.where(used, jnp.minimum(length - offset, PAGE), 0)
    inner = jnp.arange(PAGE, dtype=jnp.int32)
    rows = (source[:, None] + inner[None, :]).reshape(-1)
    keep = (inner[None, :] < valid[:, None]).reshape(-1)
    rows = jnp.clip(rows, 0, TOK_DEV - 1)
    return rows, keep


def gather_rows(hidden, row_size):
    chips = row_size // 2
    assert chips == 4
    tokens, width = hidden.shape
    index = lax.axis_index("row")
    core = index % 2
    chip = index // 2
    step = 2 * core - 1
    swap = [(i, i ^ 1) for i in range(row_size)]
    ring = [
        (i, ((i // 2 + 1) % chips) * 2 if i % 2 == 0 else ((i // 2 - 1) % chips) * 2 + 1)
        for i in range(row_size)
    ]
    partner = lax.ppermute(hidden, "row", swap)
    own_block = jnp.where(
        core == 0,
        jnp.concatenate([hidden, partner], axis=1),
        jnp.concatenate([partner, hidden], axis=1),
    )
    near = lax.ppermute(own_block, "row", ring)
    half = tokens // 2
    forwarded = lax.dynamic_slice_in_dim(near, core * half, half, 0)
    far_half = lax.ppermute(forwarded, "row", ring)
    from_partner, far_other = lax.ppermute((near, far_half), "row", swap)
    first = core == 0
    after = jnp.where(first, from_partner, near)
    before = jnp.where(first, near, from_partner)
    far = jnp.where(
        first,
        jnp.concatenate([far_half, far_other], axis=0),
        jnp.concatenate([far_other, far_half], axis=0),
    )
    blocks = []
    for k in range(chips):
        relative = (k - chip) % chips
        blocks.append(
            jnp.where(
                relative == 0,
                own_block,
                jnp.where(relative == 1, after, jnp.where(relative == 2, far, before)),
            )
        )
    full = jnp.concatenate(blocks, axis=1)
    return full


def shards(
    hidden,
    w_query,
    w_key,
    w_value,
    adapter_down,
    adapter_up_query,
    adapter_up_value,
    lengths,
    request_adapter,
    adapter_slot,
    page_table,
):
    lengths = lengths[0]
    chosen_request = jnp.take(adapter_slot, request_adapter[0])
    starts, position, chosen = token_layout(lengths, chosen_request)
    adapter_count = adapter_slot.shape[0]
    rank_width = adapter_up_query.shape[1]
    query_width = w_query.shape[1]
    key_width = w_key.shape[1]

    weight_width = query_width + 2 * key_width
    feature_rows = w_query.shape[0]
    down_shape = adapter_down.shape[1:]
    row_size = lax.axis_size("row")

    col_size = lax.axis_size("col")
    col_index = lax.axis_index("col")

    with jax.named_scope("gathers"):
        full_rows = gather_rows(hidden, row_size)
        weights = lax.all_gather(
            jnp.concatenate([w_query, w_key, w_value], axis=1), "col", axis=0, tiled=True
        )
        factors = (adapter_down, adapter_up_query, adapter_up_value)
        distance = 1
        while distance < col_size:
            pairs = [(i, i ^ distance) for i in range(col_size)]
            received = lax.ppermute(factors, "col", pairs)
            factors = tuple(
                jnp.concatenate([mine, theirs], axis=0) for mine, theirs in zip(factors, received)
            )
            distance *= 2
        down_local, up_query, up_value = factors

    with jax.named_scope("lowrank"):
        relative_slot = jnp.bitwise_xor(chosen, col_index)
        onehot = relative_slot[:, None] == jnp.arange(adapter_count, dtype=jnp.int32)[None, :]
        partial_all = jnp.einsum(
            "tf,sfr->tsr", hidden, down_local, preferred_element_type=jnp.float32
        )
        partial = jnp.sum(jnp.where(onehot[:, :, None], partial_all, 0.0), axis=1)
        distance = 1
        while distance < row_size:
            pairs = [(i, i ^ distance) for i in range(row_size)]
            partial = partial + lax.ppermute(partial, "row", pairs)
            distance *= 2
        lowrank = partial.astype(jnp.bfloat16)
        onehot_b = onehot.astype(jnp.bfloat16)
        spread_query = (onehot_b[:, :, None] * lowrank[:, None, :rank_width]).reshape(
            -1, adapter_count * rank_width
        )
        spread_value = (onehot_b[:, :, None] * lowrank[:, None, rank_width:]).reshape(
            -1, adapter_count * rank_width
        )
        delta_query = jnp.dot(
            spread_query,
            up_query.reshape(adapter_count * rank_width, -1),
            preferred_element_type=jnp.float32,
        )
        delta_value = jnp.dot(
            spread_value,
            up_value.reshape(adapter_count * rank_width, -1),
            preferred_element_type=jnp.float32,
        )

    with jax.named_scope("projection"):
        base = jnp.dot(full_rows, weights, preferred_element_type=jnp.float32)
        base_query = base[:, :query_width]
        base_key = base[:, query_width : query_width + key_width]
        base_value = base[:, query_width + key_width :]

    with jax.named_scope("rotary"):
        half_width = HEAD // 2
        frequency = jnp.exp(
            jnp.arange(half_width, dtype=jnp.float32) * (-2.0 * math.log(10000.0) / HEAD)
        )
        angles = position.astype(jnp.float32)[:, None] * frequency[None, :]
        cosine = jnp.cos(angles)[:, None, :]
        sine_value = jnp.sin(angles)[:, None, :]
        query = rotate(base_query + delta_query, cosine, sine_value).astype(jnp.bfloat16)
        key_rotated = rotate(base_key, cosine, sine_value).astype(jnp.bfloat16)
        value_rows = (base_value + delta_value).astype(jnp.bfloat16)

    with jax.named_scope("cache_write"):
        pages = page_table.shape[1]
        rows, keep = cache_rows(lengths, starts, page_table[0])
        select = (
            (rows[:, None] == jnp.arange(TOK_DEV, dtype=jnp.int32)[None, :]) & keep[:, None]
        ).astype(jnp.bfloat16)
        both = jnp.dot(
            select,
            jnp.concatenate([key_rotated, value_rows], axis=1),
            preferred_element_type=jnp.float32,
        ).astype(jnp.bfloat16)
        key_cache = both[:, :key_width].reshape(pages, PAGE, key_width)
        value_cache = both[:, key_width:].reshape(pages, PAGE, key_width)
    return (query, key_cache.astype(jnp.bfloat16), value_cache.astype(jnp.bfloat16))


def solution(mesh):
    return jax.shard_map(
        shards,
        mesh=mesh,
        in_specs=(
            P("col", "row"),
            P("col", "row"),
            P("col", "row"),
            P("col", "row"),
            P("col", "row", None),
            P("col", None, "row"),
            P("col", None, "row"),
            P("col", None),
            P("col", None),
            P(),
            P("col", None),
        ),
        out_specs=(P("col", "row"), P("col", None, "row"), P("col", None, "row")),
        check_vma=False,
    )
```

```python
import math

import jax
import jax.numpy as jnp
from jax import lax
from jax.sharding import PartitionSpec as P

HEAD = 128
PAGE = 128
TOK_DEV = 1024


def rotate(values, cosine, sine_value):
    half_width = HEAD // 2
    shaped = values.reshape(values.shape[0], -1, HEAD)
    leading = shaped[:, :, :half_width]
    second = shaped[:, :, half_width:]
    rotated = jnp.concatenate(
        [leading * cosine - second * sine_value, second * cosine + leading * sine_value], axis=2
    )
    return rotated.reshape(values.shape)


def token_layout(lengths, chosen_request):
    token_index = jnp.arange(TOK_DEV, dtype=jnp.int32)
    starts = jnp.cumsum(lengths) - lengths
    inside = (token_index[:, None] >= starts[None, :]) & (
        token_index[:, None] < (starts + lengths)[None, :]
    )
    inside = inside.astype(jnp.int32)
    position = token_index - jnp.sum(inside * starts[None, :], axis=1)
    chosen = jnp.sum(inside * chosen_request[None, :], axis=1)
    return starts, position, chosen


def cache_rows(lengths, starts, page_row):
    pages = page_row.shape[0]
    pages_each = (lengths + PAGE - 1) // PAGE
    page_start = jnp.cumsum(pages_each) - pages_each
    page_ids = jnp.arange(pages, dtype=jnp.int32)
    owner = (page_row[:, None] == page_ids[None, :]).astype(jnp.int32)
    page_of_slot = jnp.sum(owner * page_ids[:, None], axis=0)
    member = (page_of_slot[:, None] >= page_start[None, :]) & (
        page_of_slot[:, None] < (page_start + pages_each)[None, :]
    )
    member = member.astype(jnp.int32)
    used = jnp.sum(member, axis=1) > 0
    first_page = jnp.sum(member * page_start[None, :], axis=1)
    first_token = jnp.sum(member * starts[None, :], axis=1)
    length = jnp.sum(member * lengths[None, :], axis=1)
    offset = (page_of_slot - first_page) * PAGE
    source = first_token + offset
    valid = jnp.where(used, jnp.minimum(length - offset, PAGE), 0)
    inner = jnp.arange(PAGE, dtype=jnp.int32)
    rows = (source[:, None] + inner[None, :]).reshape(-1)
    keep = (inner[None, :] < valid[:, None]).reshape(-1)
    rows = jnp.clip(rows, 0, TOK_DEV - 1)
    return rows, keep


def gather_rows(hidden, row_size):
    chips = row_size // 2
    assert chips == 4
    tokens, width = hidden.shape
    index = lax.axis_index("row")
    core = index % 2
    chip = index // 2
    step = 2 * core - 1
    swap = [(i, i ^ 1) for i in range(row_size)]
    ring = [
        (i, ((i // 2 + 1) % chips) * 2 if i % 2 == 0 else ((i // 2 - 1) % chips) * 2 + 1)
        for i in range(row_size)
    ]
    partner = lax.ppermute(hidden, "row", swap)
    own_block = jnp.where(
        core == 0,
        jnp.concatenate([hidden, partner], axis=1),
        jnp.concatenate([partner, hidden], axis=1),
    )
    near = lax.ppermute(own_block, "row", ring)
    half = tokens // 2
    forwarded = lax.dynamic_slice_in_dim(near, core * half, half, 0)
    far_half = lax.ppermute(forwarded, "row", ring)
    from_partner, far_other = lax.ppermute((near, far_half), "row", swap)
    first = core == 0
    after = jnp.where(first, from_partner, near)
    before = jnp.where(first, near, from_partner)
    far = jnp.where(
        first,
        jnp.concatenate([far_half, far_other], axis=0),
        jnp.concatenate([far_other, far_half], axis=0),
    )
    blocks = []
    for k in range(chips):
        relative = (k - chip) % chips
        blocks.append(
            jnp.where(
                relative == 0,
                own_block,
                jnp.where(relative == 1, after, jnp.where(relative == 2, far, before)),
            )
        )
    full = jnp.concatenate(blocks, axis=1)
    return full


def shards(
    hidden,
    w_query,
    w_key,
    w_value,
    adapter_down,
    adapter_up_query,
    adapter_up_value,
    lengths,
    request_adapter,
    adapter_slot,
    page_table,
):
    lengths = lengths[0]
    chosen_request = jnp.take(adapter_slot, request_adapter[0])
    starts, position, chosen = token_layout(lengths, chosen_request)
    adapter_count = adapter_slot.shape[0]
    rank_width = adapter_up_query.shape[1]
    query_width = w_query.shape[1]
    key_width = w_key.shape[1]

    weight_width = query_width + 2 * key_width
    feature_rows = w_query.shape[0]
    down_shape = adapter_down.shape[1:]
    row_size = lax.axis_size("row")

    with jax.named_scope("gathers"):
        full_rows = gather_rows(hidden, row_size)
        features = down_shape[0]
        down_rows = jnp.pad(
            jnp.transpose(adapter_down[0]), ((0, 0), (0, weight_width - features))
        )
        pieces = [
            jnp.concatenate([w_query, w_key, w_value], axis=1),
            down_rows,
            adapter_up_query.reshape(-1, weight_width),
            adapter_up_value.reshape(-1, weight_width),
        ]
        pieces = [jnp.pad(p, ((0, -p.shape[0] % 8), (0, 0))) for p in pieces]
        bounds = [0]
        for piece in pieces:
            bounds.append(bounds[-1] + piece.shape[0])
        packed = lax.all_gather(jnp.concatenate(pieces, axis=0), "col", axis=0)
        weights = packed[:, :feature_rows]
        down_local = packed[:, bounds[1] : bounds[2]].reshape(-1, weight_width)
        up_query = packed[:, bounds[2] : bounds[3]].reshape(adapter_count, -1)
        up_query = up_query[:, : rank_width * query_width].reshape(adapter_count, rank_width, -1)
        up_value = packed[:, bounds[3] : bounds[4]].reshape(adapter_count, -1)
        up_value = up_value[:, : rank_width * key_width].reshape(adapter_count, rank_width, -1)

    with jax.named_scope("lowrank"):
        onehot = (chosen[:, None] == jnp.arange(adapter_count, dtype=jnp.int32)[None, :])
        padded_hidden = jnp.pad(hidden, ((0, 0), (0, weight_width - features)))
        partial_all = lax.dot_general(
            padded_hidden,
            down_local,
            (((1,), (1,)), ((), ())),
            preferred_element_type=jnp.float32,
        ).reshape(hidden.shape[0], adapter_count, -1)
        partial = jnp.sum(jnp.where(onehot[:, :, None], partial_all, 0.0), axis=1)
        partial, full_rows, packed = lax.optimization_barrier((partial, full_rows, packed))
        distance = 1
        while distance < row_size:
            pairs = [(i, i ^ distance) for i in range(row_size)]
            partial = partial + lax.ppermute(partial, "row", pairs)
            distance *= 2
        lowrank = partial.astype(jnp.bfloat16)
        onehot_b = onehot.astype(jnp.bfloat16)
        spread_query = (onehot_b[:, :, None] * lowrank[:, None, :rank_width]).reshape(
            -1, adapter_count * rank_width
        )
        spread_value = (onehot_b[:, :, None] * lowrank[:, None, rank_width:]).reshape(
            -1, adapter_count * rank_width
        )
        delta_query = jnp.dot(
            spread_query,
            up_query.reshape(adapter_count * rank_width, -1),
            preferred_element_type=jnp.float32,
        )
        delta_value = jnp.dot(
            spread_value,
            up_value.reshape(adapter_count * rank_width, -1),
            preferred_element_type=jnp.float32,
        )

    with jax.named_scope("projection"):
        stacked_rows = full_rows.reshape(full_rows.shape[0], packed.shape[0], feature_rows)
        bases = []
        for first, last in (
            (0, query_width),
            (query_width, query_width + key_width),
            (query_width + key_width, weight_width),
        ):
            bases.append(
                jnp.einsum(
                    "tci,cin->tn",
                    stacked_rows,
                    packed[:, :feature_rows, first:last],
                    preferred_element_type=jnp.float32,
                )
            )
        base_query, base_key, base_value = lax.optimization_barrier(tuple(bases))

    with jax.named_scope("rotary"):
        half_width = HEAD // 2
        frequency = jnp.exp(
            jnp.arange(half_width, dtype=jnp.float32) * (-2.0 * math.log(10000.0) / HEAD)
        )
        angles = position.astype(jnp.float32)[:, None] * frequency[None, :]
        cosine = jnp.cos(angles)[:, None, :]
        sine_value = jnp.sin(angles)[:, None, :]
        query = rotate(base_query + delta_query, cosine, sine_value).astype(jnp.bfloat16)
        key_rotated = rotate(base_key, cosine, sine_value).astype(jnp.bfloat16)
        value_rows = (base_value + delta_value).astype(jnp.bfloat16)

    with jax.named_scope("cache_write"):
        pages = page_table.shape[1]
        rows, keep = cache_rows(lengths, starts, page_table[0])
        select = (
            (rows[:, None] == jnp.arange(TOK_DEV, dtype=jnp.int32)[None, :]) & keep[:, None]
        ).astype(jnp.bfloat16)
        both = jnp.dot(
            select,
            jnp.concatenate([key_rotated, value_rows], axis=1),
            preferred_element_type=jnp.float32,
        ).astype(jnp.bfloat16)
        key_cache = both[:, :key_width].reshape(pages, PAGE, key_width)
        value_cache = both[:, key_width:].reshape(pages, PAGE, key_width)
    return (query, key_cache.astype(jnp.bfloat16), value_cache.astype(jnp.bfloat16))


def solution(mesh):
    return jax.shard_map(
        shards,
        mesh=mesh,
        in_specs=(
            P("col", "row"),
            P("col", "row"),
            P("col", "row"),
            P("col", "row"),
            P("col", "row", None),
            P("col", None, "row"),
            P("col", None, "row"),
            P("col", None),
            P("col", None),
            P(),
            P("col", None),
        ),
        out_specs=(P("col", "row"), P("col", None, "row"), P("col", None, "row")),
        check_vma=False,
    )
```

```python
import math

import jax
import jax.numpy as jnp
from jax import lax
from jax.sharding import PartitionSpec as P

HEAD = 128
PAGE = 128
TOK_DEV = 1024


def rotate(values, cosine, sine_value):
    half_width = HEAD // 2
    shaped = values.reshape(values.shape[0], -1, HEAD)
    leading = shaped[:, :, :half_width]
    second = shaped[:, :, half_width:]
    rotated = jnp.concatenate(
        [leading * cosine - second * sine_value, second * cosine + leading * sine_value], axis=2
    )
    return rotated.reshape(values.shape)


def token_layout(lengths, chosen_request):
    token_index = jnp.arange(TOK_DEV, dtype=jnp.int32)
    starts = jnp.cumsum(lengths) - lengths
    inside = (token_index[:, None] >= starts[None, :]) & (
        token_index[:, None] < (starts + lengths)[None, :]
    )
    inside = inside.astype(jnp.int32)
    position = token_index - jnp.sum(inside * starts[None, :], axis=1)
    chosen = jnp.sum(inside * chosen_request[None, :], axis=1)
    return starts, position, chosen


def cache_rows(lengths, starts, page_row):
    pages = page_row.shape[0]
    pages_each = (lengths + PAGE - 1) // PAGE
    page_start = jnp.cumsum(pages_each) - pages_each
    page_ids = jnp.arange(pages, dtype=jnp.int32)
    owner = (page_row[:, None] == page_ids[None, :]).astype(jnp.int32)
    page_of_slot = jnp.sum(owner * page_ids[:, None], axis=0)
    member = (page_of_slot[:, None] >= page_start[None, :]) & (
        page_of_slot[:, None] < (page_start + pages_each)[None, :]
    )
    member = member.astype(jnp.int32)
    used = jnp.sum(member, axis=1) > 0
    first_page = jnp.sum(member * page_start[None, :], axis=1)
    first_token = jnp.sum(member * starts[None, :], axis=1)
    length = jnp.sum(member * lengths[None, :], axis=1)
    offset = (page_of_slot - first_page) * PAGE
    source = first_token + offset
    valid = jnp.where(used, jnp.minimum(length - offset, PAGE), 0)
    inner = jnp.arange(PAGE, dtype=jnp.int32)
    rows = (source[:, None] + inner[None, :]).reshape(-1)
    keep = (inner[None, :] < valid[:, None]).reshape(-1)
    rows = jnp.clip(rows, 0, TOK_DEV - 1)
    return rows, keep


def gather_rows(hidden, row_size):
    chips = row_size // 2
    assert chips == 4
    tokens, width = hidden.shape
    index = lax.axis_index("row")
    core = index % 2
    chip = index // 2
    step = 2 * core - 1
    swap = [(i, i ^ 1) for i in range(row_size)]
    ring = [
        (i, ((i // 2 + 1) % chips) * 2 if i % 2 == 0 else ((i // 2 - 1) % chips) * 2 + 1)
        for i in range(row_size)
    ]
    partner = lax.ppermute(hidden, "row", swap)
    own_block = jnp.where(
        core == 0,
        jnp.concatenate([hidden, partner], axis=1),
        jnp.concatenate([partner, hidden], axis=1),
    )
    near = lax.ppermute(own_block, "row", ring)
    half = tokens // 2
    forwarded = lax.dynamic_slice_in_dim(near, core * half, half, 0)
    far_half = lax.ppermute(forwarded, "row", ring)
    from_partner, far_other = lax.ppermute((near, far_half), "row", swap)
    first = core == 0
    after = jnp.where(first, from_partner, near)
    before = jnp.where(first, near, from_partner)
    far = jnp.where(
        first,
        jnp.concatenate([far_half, far_other], axis=0),
        jnp.concatenate([far_other, far_half], axis=0),
    )
    blocks = []
    for k in range(chips):
        relative = (k - chip) % chips
        blocks.append(
            jnp.where(
                relative == 0,
                own_block,
                jnp.where(relative == 1, after, jnp.where(relative == 2, far, before)),
            )
        )
    full = jnp.concatenate(blocks, axis=1)
    return full


def shards(
    hidden,
    w_query,
    w_key,
    w_value,
    adapter_down,
    adapter_up_query,
    adapter_up_value,
    lengths,
    request_adapter,
    adapter_slot,
    page_table,
):
    lengths = lengths[0]
    chosen_request = jnp.take(adapter_slot, request_adapter[0])
    starts, position, chosen = token_layout(lengths, chosen_request)
    adapter_count = adapter_slot.shape[0]
    rank_width = adapter_up_query.shape[1]
    query_width = w_query.shape[1]
    key_width = w_key.shape[1]

    weight_width = query_width + 2 * key_width
    feature_rows = w_query.shape[0]
    down_shape = adapter_down.shape[1:]
    row_size = lax.axis_size("row")

    with jax.named_scope("gathers"):
        full_rows = gather_rows(hidden, row_size)
        features = down_shape[0]
        down_rows = jnp.pad(
            jnp.transpose(adapter_down[0]), ((0, 0), (0, weight_width - features))
        )
        pieces = [
            jnp.concatenate([w_query, w_key, w_value], axis=1),
            down_rows,
            adapter_up_query.reshape(-1, weight_width),
            adapter_up_value.reshape(-1, weight_width),
        ]
        pieces = [jnp.pad(p, ((0, -p.shape[0] % 8), (0, 0))) for p in pieces]
        bounds = [0]
        for piece in pieces:
            bounds.append(bounds[-1] + piece.shape[0])
        packed = lax.all_gather(jnp.concatenate(pieces, axis=0), "col", axis=0)
        weights = packed[:, :feature_rows]
        down_local = packed[:, bounds[1] : bounds[2]].reshape(-1, weight_width)
        up_query = packed[:, bounds[2] : bounds[3]].reshape(adapter_count, -1)
        up_query = up_query[:, : rank_width * query_width].reshape(adapter_count, rank_width, -1)
        up_value = packed[:, bounds[3] : bounds[4]].reshape(adapter_count, -1)
        up_value = up_value[:, : rank_width * key_width].reshape(adapter_count, rank_width, -1)

    with jax.named_scope("lowrank"):
        onehot = (chosen[:, None] == jnp.arange(adapter_count, dtype=jnp.int32)[None, :])
        padded_hidden = jnp.pad(hidden, ((0, 0), (0, weight_width - features)))
        partial_all = lax.dot_general(
            padded_hidden,
            down_local,
            (((1,), (1,)), ((), ())),
            preferred_element_type=jnp.float32,
        ).reshape(hidden.shape[0], adapter_count, -1)
        partial = jnp.sum(jnp.where(onehot[:, :, None], partial_all, 0.0), axis=1)
        partial, full_rows = lax.optimization_barrier((partial, full_rows))
        distance = 1
        while distance < row_size:
            pairs = [(i, i ^ distance) for i in range(row_size)]
            partial = partial + lax.ppermute(partial, "row", pairs)
            distance *= 2
        lowrank = partial.astype(jnp.bfloat16)
        onehot_b = onehot.astype(jnp.bfloat16)
        spread_query = (onehot_b[:, :, None] * lowrank[:, None, :rank_width]).reshape(
            -1, adapter_count * rank_width
        )
        spread_value = (onehot_b[:, :, None] * lowrank[:, None, rank_width:]).reshape(
            -1, adapter_count * rank_width
        )
        delta_query = jnp.dot(
            spread_query,
            up_query.reshape(adapter_count * rank_width, -1),
            preferred_element_type=jnp.float32,
        )
        delta_value = jnp.dot(
            spread_value,
            up_value.reshape(adapter_count * rank_width, -1),
            preferred_element_type=jnp.float32,
        )

    with jax.named_scope("projection"):
        base = jnp.einsum(
            "tci,cin->tn",
            full_rows.reshape(full_rows.shape[0], packed.shape[0], feature_rows),
            weights,
            preferred_element_type=jnp.float32,
        )
        base_query = base[:, :query_width]
        base_key = base[:, query_width : query_width + key_width]
        base_value = base[:, query_width + key_width :]

    with jax.named_scope("rotary"):
        half_width = HEAD // 2
        frequency = jnp.exp(
            jnp.arange(half_width, dtype=jnp.float32) * (-2.0 * math.log(10000.0) / HEAD)
        )
        angles = position.astype(jnp.float32)[:, None] * frequency[None, :]
        cosine = jnp.cos(angles)[:, None, :]
        sine_value = jnp.sin(angles)[:, None, :]
        query = rotate(base_query + delta_query, cosine, sine_value).astype(jnp.bfloat16)
        key_rotated = rotate(base_key, cosine, sine_value).astype(jnp.bfloat16)
        value_rows = (base_value + delta_value).astype(jnp.bfloat16)

    with jax.named_scope("cache_write"):
        pages = page_table.shape[1]
        rows, keep = cache_rows(lengths, starts, page_table[0])
        select = (
            (rows[:, None] == jnp.arange(TOK_DEV, dtype=jnp.int32)[None, :]) & keep[:, None]
        ).astype(jnp.bfloat16)
        key_cache = jnp.dot(select, key_rotated, preferred_element_type=jnp.float32)
        key_cache = key_cache.astype(jnp.bfloat16).reshape(pages, PAGE, key_width)
        value_cache = jnp.dot(select, value_rows, preferred_element_type=jnp.float32)
        value_cache = value_cache.astype(jnp.bfloat16).reshape(pages, PAGE, key_width)
    return (query, key_cache.astype(jnp.bfloat16), value_cache.astype(jnp.bfloat16))


def solution(mesh):
    return jax.shard_map(
        shards,
        mesh=mesh,
        in_specs=(
            P("col", "row"),
            P("col", "row"),
            P("col", "row"),
            P("col", "row"),
            P("col", "row", None),
            P("col", None, "row"),
            P("col", None, "row"),
            P("col", None),
            P("col", None),
            P(),
            P("col", None),
        ),
        out_specs=(P("col", "row"), P("col", None, "row"), P("col", None, "row")),
        check_vma=False,
    )
```

```python
import math

import jax
import jax.numpy as jnp
from jax import lax
from jax.sharding import PartitionSpec as P

HEAD = 128
PAGE = 128
TOK_DEV = 1024


def rotate(values, cosine, sine_value):
    half_width = HEAD // 2
    shaped = values.reshape(values.shape[0], -1, HEAD)
    leading = shaped[:, :, :half_width]
    second = shaped[:, :, half_width:]
    rotated = jnp.concatenate(
        [leading * cosine - second * sine_value, second * cosine + leading * sine_value], axis=2
    )
    return rotated.reshape(values.shape)


def token_layout(lengths, chosen_request):
    token_index = jnp.arange(TOK_DEV, dtype=jnp.int32)
    starts = jnp.cumsum(lengths) - lengths
    inside = (token_index[:, None] >= starts[None, :]) & (
        token_index[:, None] < (starts + lengths)[None, :]
    )
    inside = inside.astype(jnp.int32)
    position = token_index - jnp.sum(inside * starts[None, :], axis=1)
    chosen = jnp.sum(inside * chosen_request[None, :], axis=1)
    return starts, position, chosen


def cache_rows(lengths, starts, page_row):
    pages = page_row.shape[0]
    pages_each = (lengths + PAGE - 1) // PAGE
    page_start = jnp.cumsum(pages_each) - pages_each
    page_ids = jnp.arange(pages, dtype=jnp.int32)
    owner = (page_row[:, None] == page_ids[None, :]).astype(jnp.int32)
    page_of_slot = jnp.sum(owner * page_ids[:, None], axis=0)
    member = (page_of_slot[:, None] >= page_start[None, :]) & (
        page_of_slot[:, None] < (page_start + pages_each)[None, :]
    )
    member = member.astype(jnp.int32)
    used = jnp.sum(member, axis=1) > 0
    first_page = jnp.sum(member * page_start[None, :], axis=1)
    first_token = jnp.sum(member * starts[None, :], axis=1)
    length = jnp.sum(member * lengths[None, :], axis=1)
    offset = (page_of_slot - first_page) * PAGE
    source = first_token + offset
    valid = jnp.where(used, jnp.minimum(length - offset, PAGE), 0)
    inner = jnp.arange(PAGE, dtype=jnp.int32)
    rows = (source[:, None] + inner[None, :]).reshape(-1)
    keep = (inner[None, :] < valid[:, None]).reshape(-1)
    rows = jnp.clip(rows, 0, TOK_DEV - 1)
    return rows, keep


def gather_rows(hidden, row_size):
    chips = row_size // 2
    assert chips == 4
    tokens, width = hidden.shape
    index = lax.axis_index("row")
    core = index % 2
    chip = index // 2
    step = 2 * core - 1
    swap = [(i, i ^ 1) for i in range(row_size)]
    ring = [
        (i, ((i // 2 + 1) % chips) * 2 if i % 2 == 0 else ((i // 2 - 1) % chips) * 2 + 1)
        for i in range(row_size)
    ]
    partner = lax.ppermute(hidden, "row", swap)
    own_block = jnp.where(
        core == 0,
        jnp.concatenate([hidden, partner], axis=1),
        jnp.concatenate([partner, hidden], axis=1),
    )
    near = lax.ppermute(own_block, "row", ring)
    half = tokens // 2
    forwarded = lax.dynamic_slice_in_dim(near, core * half, half, 0)
    far_half = lax.ppermute(forwarded, "row", ring)
    from_partner, far_other = lax.ppermute((near, far_half), "row", swap)
    first = core == 0
    after = jnp.where(first, from_partner, near)
    before = jnp.where(first, near, from_partner)
    far = jnp.where(
        first,
        jnp.concatenate([far_half, far_other], axis=0),
        jnp.concatenate([far_other, far_half], axis=0),
    )
    blocks = []
    for k in range(chips):
        relative = (k - chip) % chips
        blocks.append(
            jnp.where(
                relative == 0,
                own_block,
                jnp.where(relative == 1, after, jnp.where(relative == 2, far, before)),
            )
        )
    full = jnp.concatenate(blocks, axis=1)
    return full


def shards(
    hidden,
    w_query,
    w_key,
    w_value,
    adapter_down,
    adapter_up_query,
    adapter_up_value,
    lengths,
    request_adapter,
    adapter_slot,
    page_table,
):
    lengths = lengths[0]
    chosen_request = jnp.take(adapter_slot, request_adapter[0])
    starts, position, chosen = token_layout(lengths, chosen_request)
    adapter_count = adapter_slot.shape[0]
    rank_width = adapter_up_query.shape[1]
    query_width = w_query.shape[1]
    key_width = w_key.shape[1]

    weight_width = query_width + 2 * key_width
    feature_rows = w_query.shape[0]
    down_shape = adapter_down.shape[1:]
    row_size = lax.axis_size("row")

    with jax.named_scope("gathers"):
        full_rows = gather_rows(hidden, row_size)
        features = down_shape[0]
        spare = weight_width - features
        down_t = jnp.transpose(adapter_down[0])
        up_flat = jnp.concatenate(
            [adapter_up_query.reshape(-1), adapter_up_value.reshape(-1)]
        )
        up_flat = jnp.pad(up_flat, (0, down_t.shape[0] * spare - up_flat.shape[0]))
        down_rows = jnp.concatenate([down_t, up_flat.reshape(down_t.shape[0], spare)], axis=1)
        pieces = [
            jnp.concatenate([w_query, w_key, w_value], axis=1),
            down_rows,
        ]
        pieces = [jnp.pad(p, ((0, -p.shape[0] % 8), (0, 0))) for p in pieces]
        bounds = [0]
        for piece in pieces:
            bounds.append(bounds[-1] + piece.shape[0])
        packed = lax.all_gather(jnp.concatenate(pieces, axis=0), "col", axis=0)
        weights = packed[:, :feature_rows]
        down_local = packed[:, bounds[1] : bounds[2]].reshape(-1, weight_width)
        up_all = packed[:, bounds[1] : bounds[2], features:].reshape(adapter_count, -1)
        query_size = rank_width * query_width
        up_query = up_all[:, :query_size].reshape(adapter_count, rank_width, -1)
        up_value = up_all[:, query_size : query_size + rank_width * key_width]
        up_value = up_value.reshape(adapter_count, rank_width, -1)

    with jax.named_scope("lowrank"):
        onehot = (chosen[:, None] == jnp.arange(adapter_count, dtype=jnp.int32)[None, :])
        padded_hidden = jnp.pad(hidden, ((0, 0), (0, weight_width - features)))
        partial_all = lax.dot_general(
            padded_hidden,
            down_local,
            (((1,), (1,)), ((), ())),
            preferred_element_type=jnp.float32,
        ).reshape(hidden.shape[0], adapter_count, -1)
        partial = jnp.sum(jnp.where(onehot[:, :, None], partial_all, 0.0), axis=1)
        partial, full_rows = lax.optimization_barrier((partial, full_rows))
        distance = 1
        while distance < row_size:
            pairs = [(i, i ^ distance) for i in range(row_size)]
            partial = partial + lax.ppermute(partial, "row", pairs)
            distance *= 2
        lowrank = partial.astype(jnp.bfloat16)
        onehot_b = onehot.astype(jnp.bfloat16)
        spread_query = (onehot_b[:, :, None] * lowrank[:, None, :rank_width]).reshape(
            -1, adapter_count * rank_width
        )
        spread_value = (onehot_b[:, :, None] * lowrank[:, None, rank_width:]).reshape(
            -1, adapter_count * rank_width
        )
        delta_query = jnp.dot(
            spread_query,
            up_query.reshape(adapter_count * rank_width, -1),
            preferred_element_type=jnp.float32,
        )
        delta_value = jnp.dot(
            spread_value,
            up_value.reshape(adapter_count * rank_width, -1),
            preferred_element_type=jnp.float32,
        )

    with jax.named_scope("projection"):
        base = jnp.einsum(
            "tci,cin->tn",
            full_rows.reshape(full_rows.shape[0], packed.shape[0], feature_rows),
            weights,
            preferred_element_type=jnp.float32,
        )
        base_query = base[:, :query_width]
        base_key = base[:, query_width : query_width + key_width]
        base_value = base[:, query_width + key_width :]

    with jax.named_scope("rotary"):
        half_width = HEAD // 2
        frequency = jnp.exp(
            jnp.arange(half_width, dtype=jnp.float32) * (-2.0 * math.log(10000.0) / HEAD)
        )
        angles = position.astype(jnp.float32)[:, None] * frequency[None, :]
        cosine = jnp.cos(angles)[:, None, :]
        sine_value = jnp.sin(angles)[:, None, :]
        query = rotate(base_query + delta_query, cosine, sine_value).astype(jnp.bfloat16)
        key_rotated = rotate(base_key, cosine, sine_value).astype(jnp.bfloat16)
        value_rows = (base_value + delta_value).astype(jnp.bfloat16)

    with jax.named_scope("cache_write"):
        pages = page_table.shape[1]
        rows, keep = cache_rows(lengths, starts, page_table[0])
        select = (
            (rows[:, None] == jnp.arange(TOK_DEV, dtype=jnp.int32)[None, :]) & keep[:, None]
        ).astype(jnp.bfloat16)
        key_cache = jnp.dot(select, key_rotated, preferred_element_type=jnp.float32)
        key_cache = key_cache.astype(jnp.bfloat16).reshape(pages, PAGE, key_width)
        value_cache = jnp.dot(select, value_rows, preferred_element_type=jnp.float32)
        value_cache = value_cache.astype(jnp.bfloat16).reshape(pages, PAGE, key_width)
    return (query, key_cache.astype(jnp.bfloat16), value_cache.astype(jnp.bfloat16))


def solution(mesh):
    return jax.shard_map(
        shards,
        mesh=mesh,
        in_specs=(
            P("col", "row"),
            P("col", "row"),
            P("col", "row"),
            P("col", "row"),
            P("col", "row", None),
            P("col", None, "row"),
            P("col", None, "row"),
            P("col", None),
            P("col", None),
            P(),
            P("col", None),
        ),
        out_specs=(P("col", "row"), P("col", None, "row"), P("col", None, "row")),
        check_vma=False,
    )
```

```python
import math

import jax
import jax.numpy as jnp
from jax import lax
from jax.sharding import PartitionSpec as P

HEAD = 128
PAGE = 128
TOK_DEV = 1024


def rotate(values, cosine, sine_value):
    half_width = HEAD // 2
    shaped = values.reshape(values.shape[0], -1, HEAD)
    leading = shaped[:, :, :half_width]
    second = shaped[:, :, half_width:]
    rotated = jnp.concatenate(
        [leading * cosine - second * sine_value, second * cosine + leading * sine_value], axis=2
    )
    return rotated.reshape(values.shape)


def token_layout(lengths, chosen_request):
    token_index = jnp.arange(TOK_DEV, dtype=jnp.int32)
    starts = jnp.cumsum(lengths) - lengths
    inside = (token_index[:, None] >= starts[None, :]) & (
        token_index[:, None] < (starts + lengths)[None, :]
    )
    inside = inside.astype(jnp.int32)
    position = token_index - jnp.sum(inside * starts[None, :], axis=1)
    chosen = jnp.sum(inside * chosen_request[None, :], axis=1)
    return starts, position, chosen


def cache_rows(lengths, starts, page_row):
    pages = page_row.shape[0]
    pages_each = (lengths + PAGE - 1) // PAGE
    page_start = jnp.cumsum(pages_each) - pages_each
    page_ids = jnp.arange(pages, dtype=jnp.int32)
    owner = (page_row[:, None] == page_ids[None, :]).astype(jnp.int32)
    page_of_slot = jnp.sum(owner * page_ids[:, None], axis=0)
    member = (page_of_slot[:, None] >= page_start[None, :]) & (
        page_of_slot[:, None] < (page_start + pages_each)[None, :]
    )
    member = member.astype(jnp.int32)
    used = jnp.sum(member, axis=1) > 0
    first_page = jnp.sum(member * page_start[None, :], axis=1)
    first_token = jnp.sum(member * starts[None, :], axis=1)
    length = jnp.sum(member * lengths[None, :], axis=1)
    offset = (page_of_slot - first_page) * PAGE
    source = first_token + offset
    valid = jnp.where(used, jnp.minimum(length - offset, PAGE), 0)
    inner = jnp.arange(PAGE, dtype=jnp.int32)
    rows = (source[:, None] + inner[None, :]).reshape(-1)
    keep = (inner[None, :] < valid[:, None]).reshape(-1)
    rows = jnp.clip(rows, 0, TOK_DEV - 1)
    return rows, keep


def gather_rows(hidden, row_size):
    chips = row_size // 2
    assert chips == 4
    tokens, width = hidden.shape
    index = lax.axis_index("row")
    core = index % 2
    chip = index // 2
    step = 2 * core - 1
    swap = [(i, i ^ 1) for i in range(row_size)]
    ring = [
        (i, ((i // 2 + 1) % chips) * 2 if i % 2 == 0 else ((i // 2 - 1) % chips) * 2 + 1)
        for i in range(row_size)
    ]
    partner = lax.ppermute(hidden, "row", swap)
    own_block = jnp.where(
        core == 0,
        jnp.concatenate([hidden, partner], axis=1),
        jnp.concatenate([partner, hidden], axis=1),
    )
    near = lax.ppermute(own_block, "row", ring)
    half = tokens // 2
    forwarded = lax.dynamic_slice_in_dim(near, core * half, half, 0)
    far_half = lax.ppermute(forwarded, "row", ring)
    from_partner, far_other = lax.ppermute((near, far_half), "row", swap)
    first = core == 0
    after = jnp.where(first, from_partner, near)
    before = jnp.where(first, near, from_partner)
    far = jnp.where(
        first,
        jnp.concatenate([far_half, far_other], axis=0),
        jnp.concatenate([far_other, far_half], axis=0),
    )
    blocks = []
    for k in range(chips):
        relative = (k - chip) % chips
        blocks.append(
            jnp.where(
                relative == 0,
                own_block,
                jnp.where(relative == 1, after, jnp.where(relative == 2, far, before)),
            )
        )
    full = jnp.concatenate(blocks, axis=1)
    return full


def shards(
    hidden,
    w_query,
    w_key,
    w_value,
    adapter_down,
    adapter_up_query,
    adapter_up_value,
    lengths,
    request_adapter,
    adapter_slot,
    page_table,
):
    lengths = lengths[0]
    chosen_request = jnp.take(adapter_slot, request_adapter[0])
    starts, position, chosen = token_layout(lengths, chosen_request)
    adapter_count = adapter_slot.shape[0]
    rank_width = adapter_up_query.shape[1]
    query_width = w_query.shape[1]
    key_width = w_key.shape[1]

    weight_width = query_width + 2 * key_width
    feature_rows = w_query.shape[0]
    down_shape = adapter_down.shape[1:]
    row_size = lax.axis_size("row")

    with jax.named_scope("gathers"):
        full_rows = gather_rows(hidden, row_size)
        features = down_shape[0]
        spare = weight_width - features
        down_t = jnp.transpose(adapter_down[0])
        up_flat = jnp.concatenate(
            [adapter_up_query.reshape(-1), adapter_up_value.reshape(-1)]
        )
        up_flat = jnp.pad(up_flat, (0, down_t.shape[0] * spare - up_flat.shape[0]))
        down_rows = jnp.concatenate([down_t, up_flat.reshape(down_t.shape[0], spare)], axis=1)
        pieces = [
            jnp.concatenate([w_query, w_key, w_value], axis=1),
            down_rows,
        ]
        pieces = [jnp.pad(p, ((0, -p.shape[0] % 8), (0, 0))) for p in pieces]
        bounds = [0]
        for piece in pieces:
            bounds.append(bounds[-1] + piece.shape[0])
        packed = lax.all_gather(jnp.concatenate(pieces, axis=0), "col", axis=0)
        weights = packed[:, :feature_rows]
        down_local = packed[:, bounds[1] : bounds[2]].reshape(-1, weight_width)
        up_all = packed[:, bounds[1] : bounds[2], features:].reshape(adapter_count, -1)
        query_size = rank_width * query_width
        up_query = up_all[:, :query_size].reshape(adapter_count, rank_width, -1)
        up_value = up_all[:, query_size : query_size + rank_width * key_width]
        up_value = up_value.reshape(adapter_count, rank_width, -1)

    with jax.named_scope("lowrank"):
        onehot = (chosen[:, None] == jnp.arange(adapter_count, dtype=jnp.int32)[None, :])
        padded_hidden = jnp.pad(hidden, ((0, 0), (0, weight_width - features)))
        partial_all = lax.dot_general(
            padded_hidden,
            down_local,
            (((1,), (1,)), ((), ())),
            preferred_element_type=jnp.float32,
        ).reshape(hidden.shape[0], adapter_count, -1)
        partial = jnp.sum(jnp.where(onehot[:, :, None], partial_all, 0.0), axis=1)
        partial, full_rows = lax.optimization_barrier((partial, full_rows))
        distance = row_size // 2
        while distance >= 1:
            pairs = [(i, i ^ distance) for i in range(row_size)]
            partial = partial + lax.ppermute(partial, "row", pairs)
            distance //= 2
        lowrank = partial.astype(jnp.bfloat16)
        onehot_b = onehot.astype(jnp.bfloat16)
        spread_query = (onehot_b[:, :, None] * lowrank[:, None, :rank_width]).reshape(
            -1, adapter_count * rank_width
        )
        spread_value = (onehot_b[:, :, None] * lowrank[:, None, rank_width:]).reshape(
            -1, adapter_count * rank_width
        )
        delta_query = jnp.dot(
            spread_query,
            up_query.reshape(adapter_count * rank_width, -1),
            preferred_element_type=jnp.float32,
        )
        delta_value = jnp.dot(
            spread_value,
            up_value.reshape(adapter_count * rank_width, -1),
            preferred_element_type=jnp.float32,
        )

    with jax.named_scope("projection"):
        base = jnp.einsum(
            "tci,cin->tn",
            full_rows.reshape(full_rows.shape[0], packed.shape[0], feature_rows),
            weights,
            preferred_element_type=jnp.float32,
        )
        base_query = base[:, :query_width]
        base_key = base[:, query_width : query_width + key_width]
        base_value = base[:, query_width + key_width :]

    with jax.named_scope("rotary"):
        half_width = HEAD // 2
        frequency = jnp.exp(
            jnp.arange(half_width, dtype=jnp.float32) * (-2.0 * math.log(10000.0) / HEAD)
        )
        angles = position.astype(jnp.float32)[:, None] * frequency[None, :]
        cosine = jnp.cos(angles)[:, None, :]
        sine_value = jnp.sin(angles)[:, None, :]
        query = rotate(base_query + delta_query, cosine, sine_value).astype(jnp.bfloat16)
        key_rotated = rotate(base_key, cosine, sine_value).astype(jnp.bfloat16)
        value_rows = (base_value + delta_value).astype(jnp.bfloat16)

    with jax.named_scope("cache_write"):
        pages = page_table.shape[1]
        rows, keep = cache_rows(lengths, starts, page_table[0])
        select = (
            (rows[:, None] == jnp.arange(TOK_DEV, dtype=jnp.int32)[None, :]) & keep[:, None]
        ).astype(jnp.bfloat16)
        key_cache = jnp.dot(select, key_rotated, preferred_element_type=jnp.float32)
        key_cache = key_cache.astype(jnp.bfloat16).reshape(pages, PAGE, key_width)
        value_cache = jnp.dot(select, value_rows, preferred_element_type=jnp.float32)
        value_cache = value_cache.astype(jnp.bfloat16).reshape(pages, PAGE, key_width)
    return (query, key_cache.astype(jnp.bfloat16), value_cache.astype(jnp.bfloat16))


def solution(mesh):
    return jax.shard_map(
        shards,
        mesh=mesh,
        in_specs=(
            P("col", "row"),
            P("col", "row"),
            P("col", "row"),
            P("col", "row"),
            P("col", "row", None),
            P("col", None, "row"),
            P("col", None, "row"),
            P("col", None),
            P("col", None),
            P(),
            P("col", None),
        ),
        out_specs=(P("col", "row"), P("col", None, "row"), P("col", None, "row")),
        check_vma=False,
    )
```

```python
import math

import jax
import jax.numpy as jnp
from jax import lax
from jax.sharding import PartitionSpec as P

HEAD = 128
PAGE = 128
TOK_DEV = 1024


def rotate(values, cosine, sine_value):
    half_width = HEAD // 2
    shaped = values.reshape(values.shape[0], -1, HEAD)
    leading = shaped[:, :, :half_width]
    second = shaped[:, :, half_width:]
    rotated = jnp.concatenate(
        [leading * cosine - second * sine_value, second * cosine + leading * sine_value], axis=2
    )
    return rotated.reshape(values.shape)


def token_layout(lengths, chosen_request):
    token_index = jnp.arange(TOK_DEV, dtype=jnp.int32)
    starts = jnp.cumsum(lengths) - lengths
    inside = (token_index[:, None] >= starts[None, :]) & (
        token_index[:, None] < (starts + lengths)[None, :]
    )
    inside = inside.astype(jnp.int32)
    position = token_index - jnp.sum(inside * starts[None, :], axis=1)
    chosen = jnp.sum(inside * chosen_request[None, :], axis=1)
    return starts, position, chosen


def cache_rows(lengths, starts, page_row):
    pages = page_row.shape[0]
    pages_each = (lengths + PAGE - 1) // PAGE
    page_start = jnp.cumsum(pages_each) - pages_each
    page_ids = jnp.arange(pages, dtype=jnp.int32)
    owner = (page_row[:, None] == page_ids[None, :]).astype(jnp.int32)
    page_of_slot = jnp.sum(owner * page_ids[:, None], axis=0)
    member = (page_of_slot[:, None] >= page_start[None, :]) & (
        page_of_slot[:, None] < (page_start + pages_each)[None, :]
    )
    member = member.astype(jnp.int32)
    used = jnp.sum(member, axis=1) > 0
    first_page = jnp.sum(member * page_start[None, :], axis=1)
    first_token = jnp.sum(member * starts[None, :], axis=1)
    length = jnp.sum(member * lengths[None, :], axis=1)
    offset = (page_of_slot - first_page) * PAGE
    source = first_token + offset
    valid = jnp.where(used, jnp.minimum(length - offset, PAGE), 0)
    inner = jnp.arange(PAGE, dtype=jnp.int32)
    rows = (source[:, None] + inner[None, :]).reshape(-1)
    keep = (inner[None, :] < valid[:, None]).reshape(-1)
    rows = jnp.clip(rows, 0, TOK_DEV - 1)
    return rows, keep


def gather_rows(hidden, row_size):
    chips = row_size // 2
    assert chips == 4
    tokens, width = hidden.shape
    index = lax.axis_index("row")
    core = index % 2
    chip = index // 2
    step = 2 * core - 1
    swap = [(i, i ^ 1) for i in range(row_size)]
    ring = [
        (i, ((i // 2 + 1) % chips) * 2 if i % 2 == 0 else ((i // 2 - 1) % chips) * 2 + 1)
        for i in range(row_size)
    ]
    partner = lax.ppermute(hidden, "row", swap)
    own_block = jnp.where(
        core == 0,
        jnp.concatenate([hidden, partner], axis=1),
        jnp.concatenate([partner, hidden], axis=1),
    )
    near = lax.ppermute(own_block, "row", ring)
    half = tokens // 2
    forwarded = lax.dynamic_slice_in_dim(near, core * half, half, 0)
    far_half = lax.ppermute(forwarded, "row", ring)
    from_partner, far_other = lax.ppermute((near, far_half), "row", swap)
    first = core == 0
    after = jnp.where(first, from_partner, near)
    before = jnp.where(first, near, from_partner)
    far = jnp.where(
        first,
        jnp.concatenate([far_half, far_other], axis=0),
        jnp.concatenate([far_other, far_half], axis=0),
    )
    blocks = []
    for k in range(chips):
        relative = (k - chip) % chips
        blocks.append(
            jnp.where(
                relative == 0,
                own_block,
                jnp.where(relative == 1, after, jnp.where(relative == 2, far, before)),
            )
        )
    full = jnp.concatenate(blocks, axis=1)
    return full


def shards(
    hidden,
    w_query,
    w_key,
    w_value,
    adapter_down,
    adapter_up_query,
    adapter_up_value,
    lengths,
    request_adapter,
    adapter_slot,
    page_table,
):
    lengths = lengths[0]
    chosen_request = jnp.take(adapter_slot, request_adapter[0])
    starts, position, chosen = token_layout(lengths, chosen_request)
    adapter_count = adapter_slot.shape[0]
    rank_width = adapter_up_query.shape[1]
    query_width = w_query.shape[1]
    key_width = w_key.shape[1]

    weight_width = query_width + 2 * key_width
    feature_rows = w_query.shape[0]
    down_shape = adapter_down.shape[1:]
    row_size = lax.axis_size("row")

    with jax.named_scope("gathers"):
        full_rows = gather_rows(hidden, row_size)
        features = down_shape[0]
        spare = weight_width - features
        down_t = jnp.transpose(adapter_down[0])
        up_flat = jnp.concatenate(
            [adapter_up_query.reshape(-1), adapter_up_value.reshape(-1)]
        )
        up_flat = jnp.pad(up_flat, (0, down_t.shape[0] * spare - up_flat.shape[0]))
        down_rows = jnp.concatenate([down_t, up_flat.reshape(down_t.shape[0], spare)], axis=1)
        pieces = [
            jnp.concatenate([w_query, w_key, w_value], axis=1),
            down_rows,
        ]
        pieces = [jnp.pad(p, ((0, -p.shape[0] % 8), (0, 0))) for p in pieces]
        bounds = [0]
        for piece in pieces:
            bounds.append(bounds[-1] + piece.shape[0])
        packed = lax.all_gather(jnp.concatenate(pieces, axis=0), "col", axis=0)
        weights = packed[:, :feature_rows]
        down_local = packed[:, bounds[1] : bounds[2]].reshape(-1, weight_width)
        up_all = packed[:, bounds[1] : bounds[2], features:].reshape(adapter_count, -1)
        query_size = rank_width * query_width
        up_query = up_all[:, :query_size].reshape(adapter_count, rank_width, -1)
        up_value = up_all[:, query_size : query_size + rank_width * key_width]
        up_value = up_value.reshape(adapter_count, rank_width, -1)

    with jax.named_scope("lowrank"):
        onehot = (chosen[:, None] == jnp.arange(adapter_count, dtype=jnp.int32)[None, :])
        padded_hidden = jnp.pad(hidden, ((0, 0), (0, weight_width - features)))
        partial_all = lax.dot_general(
            padded_hidden,
            down_local,
            (((1,), (1,)), ((), ())),
            preferred_element_type=jnp.float32,
        ).reshape(hidden.shape[0], adapter_count, -1)
        partial = jnp.sum(jnp.where(onehot[:, :, None], partial_all, 0.0), axis=1)
        partial, full_rows = lax.optimization_barrier((partial, full_rows))
        distance = 1
        while distance < row_size:
            pairs = [(i, i ^ distance) for i in range(row_size)]
            received = lax.ppermute(partial, "row", pairs)
            if distance == 2:
                received, up_query, up_value = lax.optimization_barrier(
                    (received, up_query, up_value)
                )
            partial = partial + received
            distance *= 2
        lowrank = partial.astype(jnp.bfloat16)
        onehot_b = onehot.astype(jnp.bfloat16)
        spread_query = (onehot_b[:, :, None] * lowrank[:, None, :rank_width]).reshape(
            -1, adapter_count * rank_width
        )
        spread_value = (onehot_b[:, :, None] * lowrank[:, None, rank_width:]).reshape(
            -1, adapter_count * rank_width
        )
        delta_query = jnp.dot(
            spread_query,
            up_query.reshape(adapter_count * rank_width, -1),
            preferred_element_type=jnp.float32,
        )
        delta_value = jnp.dot(
            spread_value,
            up_value.reshape(adapter_count * rank_width, -1),
            preferred_element_type=jnp.float32,
        )

    with jax.named_scope("projection"):
        base = jnp.einsum(
            "tci,cin->tn",
            full_rows.reshape(full_rows.shape[0], packed.shape[0], feature_rows),
            weights,
            preferred_element_type=jnp.float32,
        )
        base_query = base[:, :query_width]
        base_key = base[:, query_width : query_width + key_width]
        base_value = base[:, query_width + key_width :]

    with jax.named_scope("rotary"):
        half_width = HEAD // 2
        frequency = jnp.exp(
            jnp.arange(half_width, dtype=jnp.float32) * (-2.0 * math.log(10000.0) / HEAD)
        )
        angles = position.astype(jnp.float32)[:, None] * frequency[None, :]
        cosine = jnp.cos(angles)[:, None, :]
        sine_value = jnp.sin(angles)[:, None, :]
        query = rotate(base_query + delta_query, cosine, sine_value).astype(jnp.bfloat16)
        key_rotated = rotate(base_key, cosine, sine_value).astype(jnp.bfloat16)
        value_rows = (base_value + delta_value).astype(jnp.bfloat16)

    with jax.named_scope("cache_write"):
        pages = page_table.shape[1]
        rows, keep = cache_rows(lengths, starts, page_table[0])
        select = (
            (rows[:, None] == jnp.arange(TOK_DEV, dtype=jnp.int32)[None, :]) & keep[:, None]
        ).astype(jnp.bfloat16)
        key_cache = jnp.dot(select, key_rotated, preferred_element_type=jnp.float32)
        key_cache = key_cache.astype(jnp.bfloat16).reshape(pages, PAGE, key_width)
        value_cache = jnp.dot(select, value_rows, preferred_element_type=jnp.float32)
        value_cache = value_cache.astype(jnp.bfloat16).reshape(pages, PAGE, key_width)
    return (query, key_cache.astype(jnp.bfloat16), value_cache.astype(jnp.bfloat16))


def solution(mesh):
    return jax.shard_map(
        shards,
        mesh=mesh,
        in_specs=(
            P("col", "row"),
            P("col", "row"),
            P("col", "row"),
            P("col", "row"),
            P("col", "row", None),
            P("col", None, "row"),
            P("col", None, "row"),
            P("col", None),
            P("col", None),
            P(),
            P("col", None),
        ),
        out_specs=(P("col", "row"), P("col", None, "row"), P("col", None, "row")),
        check_vma=False,
    )
```

```python
import math

import jax
import jax.numpy as jnp
from jax import lax
from jax.sharding import PartitionSpec as P

HEAD = 128
PAGE = 128
TOK_DEV = 1024


def rotate(values, cosine, sine_value):
    half_width = HEAD // 2
    shaped = values.reshape(values.shape[0], -1, HEAD)
    leading = shaped[:, :, :half_width]
    second = shaped[:, :, half_width:]
    rotated = jnp.concatenate(
        [leading * cosine - second * sine_value, second * cosine + leading * sine_value], axis=2
    )
    return rotated.reshape(values.shape)


def token_layout(lengths, chosen_request):
    token_index = jnp.arange(TOK_DEV, dtype=jnp.int32)
    starts = jnp.cumsum(lengths) - lengths
    inside = (token_index[:, None] >= starts[None, :]) & (
        token_index[:, None] < (starts + lengths)[None, :]
    )
    inside = inside.astype(jnp.int32)
    position = token_index - jnp.sum(inside * starts[None, :], axis=1)
    chosen = jnp.sum(inside * chosen_request[None, :], axis=1)
    return starts, position, chosen


def cache_rows(lengths, starts, page_row):
    pages = page_row.shape[0]
    pages_each = (lengths + PAGE - 1) // PAGE
    page_start = jnp.cumsum(pages_each) - pages_each
    page_ids = jnp.arange(pages, dtype=jnp.int32)
    owner = (page_row[:, None] == page_ids[None, :]).astype(jnp.int32)
    page_of_slot = jnp.sum(owner * page_ids[:, None], axis=0)
    member = (page_of_slot[:, None] >= page_start[None, :]) & (
        page_of_slot[:, None] < (page_start + pages_each)[None, :]
    )
    member = member.astype(jnp.int32)
    used = jnp.sum(member, axis=1) > 0
    first_page = jnp.sum(member * page_start[None, :], axis=1)
    first_token = jnp.sum(member * starts[None, :], axis=1)
    length = jnp.sum(member * lengths[None, :], axis=1)
    offset = (page_of_slot - first_page) * PAGE
    source = first_token + offset
    valid = jnp.where(used, jnp.minimum(length - offset, PAGE), 0)
    inner = jnp.arange(PAGE, dtype=jnp.int32)
    rows = (source[:, None] + inner[None, :]).reshape(-1)
    keep = (inner[None, :] < valid[:, None]).reshape(-1)
    rows = jnp.clip(rows, 0, TOK_DEV - 1)
    return rows, keep


def gather_rows(hidden, row_size):
    chips = row_size // 2
    assert chips == 4
    tokens, width = hidden.shape
    index = lax.axis_index("row")
    core = index % 2
    chip = index // 2
    step = 2 * core - 1
    swap = [(i, i ^ 1) for i in range(row_size)]
    ring = [
        (i, ((i // 2 + 1) % chips) * 2 if i % 2 == 0 else ((i // 2 - 1) % chips) * 2 + 1)
        for i in range(row_size)
    ]
    partner = lax.ppermute(hidden, "row", swap)
    own_block = jnp.where(
        core == 0,
        jnp.concatenate([hidden, partner], axis=1),
        jnp.concatenate([partner, hidden], axis=1),
    )
    near = lax.ppermute(own_block, "row", ring)
    half = tokens // 2
    forwarded = lax.dynamic_slice_in_dim(near, core * half, half, 0)
    far_half = lax.ppermute(forwarded, "row", ring)
    from_partner, far_other = lax.ppermute((near, far_half), "row", swap)
    first = core == 0
    after = jnp.where(first, from_partner, near)
    before = jnp.where(first, near, from_partner)
    far = jnp.where(
        first,
        jnp.concatenate([far_half, far_other], axis=0),
        jnp.concatenate([far_other, far_half], axis=0),
    )
    blocks = []
    for k in range(chips):
        relative = (k - chip) % chips
        blocks.append(
            jnp.where(
                relative == 0,
                own_block,
                jnp.where(relative == 1, after, jnp.where(relative == 2, far, before)),
            )
        )
    full = jnp.concatenate(blocks, axis=1)
    return full


def shards(
    hidden,
    w_query,
    w_key,
    w_value,
    adapter_down,
    adapter_up_query,
    adapter_up_value,
    lengths,
    request_adapter,
    adapter_slot,
    page_table,
):
    lengths = lengths[0]
    chosen_request = jnp.take(adapter_slot, request_adapter[0])
    starts, position, chosen = token_layout(lengths, chosen_request)
    adapter_count = adapter_slot.shape[0]
    rank_width = adapter_up_query.shape[1]
    query_width = w_query.shape[1]
    key_width = w_key.shape[1]

    weight_width = query_width + 2 * key_width
    feature_rows = w_query.shape[0]
    down_shape = adapter_down.shape[1:]
    row_size = lax.axis_size("row")

    with jax.named_scope("gathers"):
        full_rows = gather_rows(hidden, row_size)
        features = down_shape[0]
        spare = weight_width - features
        down_t = jnp.transpose(adapter_down[0])
        up_flat = jnp.concatenate(
            [adapter_up_query.reshape(-1), adapter_up_value.reshape(-1)]
        )
        up_flat = jnp.pad(up_flat, (0, down_t.shape[0] * spare - up_flat.shape[0]))
        down_rows = jnp.concatenate([down_t, up_flat.reshape(down_t.shape[0], spare)], axis=1)
        pieces = [
            jnp.concatenate([w_query, w_key, w_value], axis=1),
            down_rows,
        ]
        pieces = [jnp.pad(p, ((0, -p.shape[0] % 8), (0, 0))) for p in pieces]
        bounds = [0]
        for piece in pieces:
            bounds.append(bounds[-1] + piece.shape[0])
        packed = lax.all_gather(jnp.concatenate(pieces, axis=0), "col", axis=0)
        weights = packed[:, :feature_rows]
        down_local = packed[:, bounds[1] : bounds[2]].reshape(-1, weight_width)
        up_all = packed[:, bounds[1] : bounds[2], features:].reshape(adapter_count, -1)
        query_size = rank_width * query_width
        up_query = up_all[:, :query_size].reshape(adapter_count, rank_width, -1)
        up_value = up_all[:, query_size : query_size + rank_width * key_width]
        up_value = up_value.reshape(adapter_count, rank_width, -1)

    with jax.named_scope("lowrank"):
        onehot = (chosen[:, None] == jnp.arange(adapter_count, dtype=jnp.int32)[None, :])
        lane_width = -(-features // 128) * 128
        padded_hidden = jnp.pad(hidden, ((0, 0), (0, lane_width - features)))
        partial_all = lax.dot_general(
            padded_hidden,
            down_local[:, :lane_width],
            (((1,), (1,)), ((), ())),
            preferred_element_type=jnp.float32,
        ).reshape(hidden.shape[0], adapter_count, -1)
        partial = jnp.sum(jnp.where(onehot[:, :, None], partial_all, 0.0), axis=1)
        partial, full_rows = lax.optimization_barrier((partial, full_rows))
        distance = 1
        while distance < row_size:
            pairs = [(i, i ^ distance) for i in range(row_size)]
            received = lax.ppermute(partial, "row", pairs)
            if distance == 2:
                received, up_query, up_value = lax.optimization_barrier(
                    (received, up_query, up_value)
                )
            partial = partial + received
            distance *= 2
        lowrank = partial.astype(jnp.bfloat16)
        onehot_b = onehot.astype(jnp.bfloat16)
        spread_query = (onehot_b[:, :, None] * lowrank[:, None, :rank_width]).reshape(
            -1, adapter_count * rank_width
        )
        spread_value = (onehot_b[:, :, None] * lowrank[:, None, rank_width:]).reshape(
            -1, adapter_count * rank_width
        )
        delta_query = jnp.dot(
            spread_query,
            up_query.reshape(adapter_count * rank_width, -1),
            preferred_element_type=jnp.float32,
        )
        delta_value = jnp.dot(
            spread_value,
            up_value.reshape(adapter_count * rank_width, -1),
            preferred_element_type=jnp.float32,
        )

    with jax.named_scope("projection"):
        base = jnp.einsum(
            "tci,cin->tn",
            full_rows.reshape(full_rows.shape[0], packed.shape[0], feature_rows),
            weights,
            preferred_element_type=jnp.float32,
        )
        base_query = base[:, :query_width]
        base_key = base[:, query_width : query_width + key_width]
        base_value = base[:, query_width + key_width :]

    with jax.named_scope("rotary"):
        half_width = HEAD // 2
        frequency = jnp.exp(
            jnp.arange(half_width, dtype=jnp.float32) * (-2.0 * math.log(10000.0) / HEAD)
        )
        angles = position.astype(jnp.float32)[:, None] * frequency[None, :]
        cosine = jnp.cos(angles)[:, None, :]
        sine_value = jnp.sin(angles)[:, None, :]
        query = rotate(base_query + delta_query, cosine, sine_value).astype(jnp.bfloat16)
        key_rotated = rotate(base_key, cosine, sine_value).astype(jnp.bfloat16)
        value_rows = (base_value + delta_value).astype(jnp.bfloat16)

    with jax.named_scope("cache_write"):
        pages = page_table.shape[1]
        rows, keep = cache_rows(lengths, starts, page_table[0])
        select = (
            (rows[:, None] == jnp.arange(TOK_DEV, dtype=jnp.int32)[None, :]) & keep[:, None]
        ).astype(jnp.bfloat16)
        key_cache = jnp.dot(select, key_rotated, preferred_element_type=jnp.float32)
        key_cache = key_cache.astype(jnp.bfloat16).reshape(pages, PAGE, key_width)
        value_cache = jnp.dot(select, value_rows, preferred_element_type=jnp.float32)
        value_cache = value_cache.astype(jnp.bfloat16).reshape(pages, PAGE, key_width)
    return (query, key_cache.astype(jnp.bfloat16), value_cache.astype(jnp.bfloat16))


def solution(mesh):
    return jax.shard_map(
        shards,
        mesh=mesh,
        in_specs=(
            P("col", "row"),
            P("col", "row"),
            P("col", "row"),
            P("col", "row"),
            P("col", "row", None),
            P("col", None, "row"),
            P("col", None, "row"),
            P("col", None),
            P("col", None),
            P(),
            P("col", None),
        ),
        out_specs=(P("col", "row"), P("col", None, "row"), P("col", None, "row")),
        check_vma=False,
    )
```

```python
import math

import jax
import jax.numpy as jnp
from jax import lax
from jax.sharding import PartitionSpec as P

HEAD = 128
PAGE = 128
TOK_DEV = 1024


def rotate(values, cosine, sine_value):
    half_width = HEAD // 2
    shaped = values.reshape(values.shape[0], -1, HEAD)
    leading = shaped[:, :, :half_width]
    second = shaped[:, :, half_width:]
    rotated = jnp.concatenate(
        [leading * cosine - second * sine_value, second * cosine + leading * sine_value], axis=2
    )
    return rotated.reshape(values.shape)


def token_layout(lengths, chosen_request):
    token_index = jnp.arange(TOK_DEV, dtype=jnp.int32)
    starts = jnp.cumsum(lengths) - lengths
    inside = (token_index[:, None] >= starts[None, :]) & (
        token_index[:, None] < (starts + lengths)[None, :]
    )
    inside = inside.astype(jnp.int32)
    position = token_index - jnp.sum(inside * starts[None, :], axis=1)
    chosen = jnp.sum(inside * chosen_request[None, :], axis=1)
    return starts, position, chosen


def cache_rows(lengths, starts, page_row):
    pages = page_row.shape[0]
    pages_each = (lengths + PAGE - 1) // PAGE
    page_start = jnp.cumsum(pages_each) - pages_each
    page_ids = jnp.arange(pages, dtype=jnp.int32)
    owner = (page_row[:, None] == page_ids[None, :]).astype(jnp.int32)
    page_of_slot = jnp.sum(owner * page_ids[:, None], axis=0)
    member = (page_of_slot[:, None] >= page_start[None, :]) & (
        page_of_slot[:, None] < (page_start + pages_each)[None, :]
    )
    member = member.astype(jnp.int32)
    used = jnp.sum(member, axis=1) > 0
    first_page = jnp.sum(member * page_start[None, :], axis=1)
    first_token = jnp.sum(member * starts[None, :], axis=1)
    length = jnp.sum(member * lengths[None, :], axis=1)
    offset = (page_of_slot - first_page) * PAGE
    source = first_token + offset
    valid = jnp.where(used, jnp.minimum(length - offset, PAGE), 0)
    inner = jnp.arange(PAGE, dtype=jnp.int32)
    rows = (source[:, None] + inner[None, :]).reshape(-1)
    keep = (inner[None, :] < valid[:, None]).reshape(-1)
    rows = jnp.clip(rows, 0, TOK_DEV - 1)
    return rows, keep


def gather_rows(hidden, row_size):
    chips = row_size // 2
    assert chips == 4
    tokens, width = hidden.shape
    index = lax.axis_index("row")
    core = index % 2
    chip = index // 2
    step = 2 * core - 1
    swap = [(i, i ^ 1) for i in range(row_size)]
    ring = [
        (i, ((i // 2 + 1) % chips) * 2 if i % 2 == 0 else ((i // 2 - 1) % chips) * 2 + 1)
        for i in range(row_size)
    ]
    partner = lax.ppermute(hidden, "row", swap)
    own_block = jnp.where(
        core == 0,
        jnp.concatenate([hidden, partner], axis=1),
        jnp.concatenate([partner, hidden], axis=1),
    )
    near = lax.ppermute(own_block, "row", ring)
    half = tokens // 2
    forwarded = lax.dynamic_slice_in_dim(near, core * half, half, 0)
    far_half = lax.ppermute(forwarded, "row", ring)
    from_partner, far_other = lax.ppermute((near, far_half), "row", swap)
    first = core == 0
    after = jnp.where(first, from_partner, near)
    before = jnp.where(first, near, from_partner)
    far = jnp.where(
        first,
        jnp.concatenate([far_half, far_other], axis=0),
        jnp.concatenate([far_other, far_half], axis=0),
    )
    blocks = []
    for k in range(chips):
        relative = (k - chip) % chips
        blocks.append(
            jnp.where(
                relative == 0,
                own_block,
                jnp.where(relative == 1, after, jnp.where(relative == 2, far, before)),
            )
        )
    full = jnp.concatenate(blocks, axis=1)
    return full


def shards(
    hidden,
    w_query,
    w_key,
    w_value,
    adapter_down,
    adapter_up_query,
    adapter_up_value,
    lengths,
    request_adapter,
    adapter_slot,
    page_table,
):
    lengths = lengths[0]
    chosen_request = jnp.take(adapter_slot, request_adapter[0])
    starts, position, chosen = token_layout(lengths, chosen_request)
    adapter_count = adapter_slot.shape[0]
    rank_width = adapter_up_query.shape[1]
    query_width = w_query.shape[1]
    key_width = w_key.shape[1]

    weight_width = query_width + 2 * key_width
    feature_rows = w_query.shape[0]
    down_shape = adapter_down.shape[1:]
    row_size = lax.axis_size("row")

    with jax.named_scope("gathers"):
        full_rows = gather_rows(hidden, row_size)
        features = down_shape[0]
        spare = weight_width - features
        down_t = jnp.transpose(adapter_down[0])
        up_flat = jnp.concatenate(
            [adapter_up_query.reshape(-1), adapter_up_value.reshape(-1)]
        )
        up_flat = jnp.pad(up_flat, (0, down_t.shape[0] * spare - up_flat.shape[0]))
        down_rows = jnp.concatenate([down_t, up_flat.reshape(down_t.shape[0], spare)], axis=1)
        pieces = [
            jnp.concatenate([w_query, w_key, w_value], axis=1),
            down_rows,
        ]
        pieces = [jnp.pad(p, ((0, -p.shape[0] % 8), (0, 0))) for p in pieces]
        bounds = [0]
        for piece in pieces:
            bounds.append(bounds[-1] + piece.shape[0])
        packed = lax.all_gather(jnp.concatenate(pieces, axis=0), "col", axis=0)
        weights = packed[:, :feature_rows]
        down_local = packed[:, bounds[1] : bounds[2]].reshape(-1, weight_width)
        up_all = packed[:, bounds[1] : bounds[2], features:].reshape(adapter_count, -1)
        query_size = rank_width * query_width
        up_query = up_all[:, :query_size].reshape(adapter_count, rank_width, -1)
        up_value = up_all[:, query_size : query_size + rank_width * key_width]
        up_value = up_value.reshape(adapter_count, rank_width, -1)

    with jax.named_scope("cache_select"):
        rows, keep = cache_rows(lengths, starts, page_table[0])
        select = (
            (rows[:, None] == jnp.arange(TOK_DEV, dtype=jnp.int32)[None, :]) & keep[:, None]
        ).astype(jnp.bfloat16)
        select, full_rows = lax.optimization_barrier((select, full_rows))

    with jax.named_scope("lowrank"):
        onehot = (chosen[:, None] == jnp.arange(adapter_count, dtype=jnp.int32)[None, :])
        padded_hidden = jnp.pad(hidden, ((0, 0), (0, weight_width - features)))
        partial_all = lax.dot_general(
            padded_hidden,
            down_local,
            (((1,), (1,)), ((), ())),
            preferred_element_type=jnp.float32,
        ).reshape(hidden.shape[0], adapter_count, -1)
        partial = jnp.sum(jnp.where(onehot[:, :, None], partial_all, 0.0), axis=1)
        partial, full_rows = lax.optimization_barrier((partial, full_rows))
        distance = 1
        while distance < row_size:
            pairs = [(i, i ^ distance) for i in range(row_size)]
            received = lax.ppermute(partial, "row", pairs)
            if distance == 2:
                received, up_query, up_value = lax.optimization_barrier(
                    (received, up_query, up_value)
                )
            partial = partial + received
            distance *= 2
        lowrank = partial.astype(jnp.bfloat16)
        onehot_b = onehot.astype(jnp.bfloat16)
        spread_query = (onehot_b[:, :, None] * lowrank[:, None, :rank_width]).reshape(
            -1, adapter_count * rank_width
        )
        spread_value = (onehot_b[:, :, None] * lowrank[:, None, rank_width:]).reshape(
            -1, adapter_count * rank_width
        )
        delta_query = jnp.dot(
            spread_query,
            up_query.reshape(adapter_count * rank_width, -1),
            preferred_element_type=jnp.float32,
        )
        delta_value = jnp.dot(
            spread_value,
            up_value.reshape(adapter_count * rank_width, -1),
            preferred_element_type=jnp.float32,
        )

    with jax.named_scope("projection"):
        base = jnp.einsum(
            "tci,cin->tn",
            full_rows.reshape(full_rows.shape[0], packed.shape[0], feature_rows),
            weights,
            preferred_element_type=jnp.float32,
        )
        base_query = base[:, :query_width]
        base_key = base[:, query_width : query_width + key_width]
        base_value = base[:, query_width + key_width :]

    with jax.named_scope("rotary"):
        half_width = HEAD // 2
        frequency = jnp.exp(
            jnp.arange(half_width, dtype=jnp.float32) * (-2.0 * math.log(10000.0) / HEAD)
        )
        angles = position.astype(jnp.float32)[:, None] * frequency[None, :]
        cosine = jnp.cos(angles)[:, None, :]
        sine_value = jnp.sin(angles)[:, None, :]
        query = rotate(base_query + delta_query, cosine, sine_value).astype(jnp.bfloat16)
        key_rotated = rotate(base_key, cosine, sine_value).astype(jnp.bfloat16)
        value_rows = (base_value + delta_value).astype(jnp.bfloat16)

    with jax.named_scope("cache_write"):
        pages = page_table.shape[1]
        key_cache = jnp.dot(select, key_rotated, preferred_element_type=jnp.float32)
        key_cache = key_cache.astype(jnp.bfloat16).reshape(pages, PAGE, key_width)
        value_cache = jnp.dot(select, value_rows, preferred_element_type=jnp.float32)
        value_cache = value_cache.astype(jnp.bfloat16).reshape(pages, PAGE, key_width)
    return (query, key_cache.astype(jnp.bfloat16), value_cache.astype(jnp.bfloat16))


def solution(mesh):
    return jax.shard_map(
        shards,
        mesh=mesh,
        in_specs=(
            P("col", "row"),
            P("col", "row"),
            P("col", "row"),
            P("col", "row"),
            P("col", "row", None),
            P("col", None, "row"),
            P("col", None, "row"),
            P("col", None),
            P("col", None),
            P(),
            P("col", None),
        ),
        out_specs=(P("col", "row"), P("col", None, "row"), P("col", None, "row")),
        check_vma=False,
    )
```

```python
import math

import jax
import jax.numpy as jnp
from jax import lax
from jax.sharding import PartitionSpec as P

HEAD = 128
PAGE = 128
TOK_DEV = 1024


def rotate(values, cosine, sine_value):
    half_width = HEAD // 2
    shaped = values.reshape(values.shape[0], -1, HEAD)
    leading = shaped[:, :, :half_width]
    second = shaped[:, :, half_width:]
    rotated = jnp.concatenate(
        [leading * cosine - second * sine_value, second * cosine + leading * sine_value], axis=2
    )
    return rotated.reshape(values.shape)


def token_layout(lengths, chosen_request):
    token_index = jnp.arange(TOK_DEV, dtype=jnp.int32)
    starts = jnp.cumsum(lengths) - lengths
    inside = (token_index[:, None] >= starts[None, :]) & (
        token_index[:, None] < (starts + lengths)[None, :]
    )
    inside = inside.astype(jnp.int32)
    position = token_index - jnp.sum(inside * starts[None, :], axis=1)
    chosen = jnp.sum(inside * chosen_request[None, :], axis=1)
    return starts, position, chosen


def cache_rows(lengths, starts, page_row):
    pages = page_row.shape[0]
    pages_each = (lengths + PAGE - 1) // PAGE
    page_start = jnp.cumsum(pages_each) - pages_each
    page_ids = jnp.arange(pages, dtype=jnp.int32)
    owner = (page_row[:, None] == page_ids[None, :]).astype(jnp.int32)
    page_of_slot = jnp.sum(owner * page_ids[:, None], axis=0)
    member = (page_of_slot[:, None] >= page_start[None, :]) & (
        page_of_slot[:, None] < (page_start + pages_each)[None, :]
    )
    member = member.astype(jnp.int32)
    used = jnp.sum(member, axis=1) > 0
    first_page = jnp.sum(member * page_start[None, :], axis=1)
    first_token = jnp.sum(member * starts[None, :], axis=1)
    length = jnp.sum(member * lengths[None, :], axis=1)
    offset = (page_of_slot - first_page) * PAGE
    source = first_token + offset
    valid = jnp.where(used, jnp.minimum(length - offset, PAGE), 0)
    inner = jnp.arange(PAGE, dtype=jnp.int32)
    rows = (source[:, None] + inner[None, :]).reshape(-1)
    keep = (inner[None, :] < valid[:, None]).reshape(-1)
    rows = jnp.clip(rows, 0, TOK_DEV - 1)
    return rows, keep


def gather_rows(hidden, row_size):
    chips = row_size // 2
    assert chips == 4
    tokens, width = hidden.shape
    index = lax.axis_index("row")
    core = index % 2
    chip = index // 2
    step = 2 * core - 1
    swap = [(i, i ^ 1) for i in range(row_size)]
    ring = [
        (i, ((i // 2 + 1) % chips) * 2 if i % 2 == 0 else ((i // 2 - 1) % chips) * 2 + 1)
        for i in range(row_size)
    ]
    partner = lax.ppermute(hidden, "row", swap)
    own_block = jnp.where(
        core == 0,
        jnp.concatenate([hidden, partner], axis=1),
        jnp.concatenate([partner, hidden], axis=1),
    )
    near = lax.ppermute(own_block, "row", ring)
    half = tokens // 2
    forwarded = lax.dynamic_slice_in_dim(near, core * half, half, 0)
    far_half = lax.ppermute(forwarded, "row", ring)
    from_partner, far_other = lax.ppermute((near, far_half), "row", swap)
    first = core == 0
    after = jnp.where(first, from_partner, near)
    before = jnp.where(first, near, from_partner)
    far = jnp.where(
        first,
        jnp.concatenate([far_half, far_other], axis=0),
        jnp.concatenate([far_other, far_half], axis=0),
    )
    blocks = []
    for k in range(chips):
        relative = (k - chip) % chips
        blocks.append(
            jnp.where(
                relative == 0,
                own_block,
                jnp.where(relative == 1, after, jnp.where(relative == 2, far, before)),
            )
        )
    full = jnp.concatenate(blocks, axis=1)
    return full


def shards(
    hidden,
    w_query,
    w_key,
    w_value,
    adapter_down,
    adapter_up_query,
    adapter_up_value,
    lengths,
    request_adapter,
    adapter_slot,
    page_table,
):
    lengths = lengths[0]
    chosen_request = jnp.take(adapter_slot, request_adapter[0])
    starts, position, chosen = token_layout(lengths, chosen_request)
    adapter_count = adapter_slot.shape[0]
    rank_width = adapter_up_query.shape[1]
    query_width = w_query.shape[1]
    key_width = w_key.shape[1]

    weight_width = query_width + 2 * key_width
    feature_rows = w_query.shape[0]
    down_shape = adapter_down.shape[1:]
    row_size = lax.axis_size("row")

    with jax.named_scope("gathers"):
        full_rows = gather_rows(hidden, row_size)
        features = down_shape[0]
        spare = weight_width - features
        down_t = jnp.transpose(adapter_down[0])
        up_flat = jnp.concatenate(
            [adapter_up_query.reshape(-1), adapter_up_value.reshape(-1)]
        )
        up_flat = jnp.pad(up_flat, (0, down_t.shape[0] * spare - up_flat.shape[0]))
        down_rows = jnp.concatenate([down_t, up_flat.reshape(down_t.shape[0], spare)], axis=1)
        pieces = [
            jnp.concatenate([w_query, w_key, w_value], axis=1),
            down_rows,
        ]
        pieces = [jnp.pad(p, ((0, -p.shape[0] % 8), (0, 0))) for p in pieces]
        bounds = [0]
        for piece in pieces:
            bounds.append(bounds[-1] + piece.shape[0])
        packed = lax.all_gather(jnp.concatenate(pieces, axis=0), "col", axis=0)
        weights = packed[:, :feature_rows]
        down_local = packed[:, bounds[1] : bounds[2]].reshape(-1, weight_width)
        up_all = packed[:, bounds[1] : bounds[2], features:].reshape(adapter_count, -1)
        query_size = rank_width * query_width
        up_query = up_all[:, :query_size].reshape(adapter_count, rank_width, -1)
        up_value = up_all[:, query_size : query_size + rank_width * key_width]
        up_value = up_value.reshape(adapter_count, rank_width, -1)

    with jax.named_scope("lowrank"):
        onehot = (chosen[:, None] == jnp.arange(adapter_count, dtype=jnp.int32)[None, :])
        padded_hidden = jnp.pad(hidden, ((0, 0), (0, weight_width - features)))
        partial_all = lax.dot_general(
            padded_hidden,
            down_local,
            (((1,), (1,)), ((), ())),
            preferred_element_type=jnp.float32,
        ).reshape(hidden.shape[0], adapter_count, -1)
        partial = jnp.sum(jnp.where(onehot[:, :, None], partial_all, 0.0), axis=1)
        partial, full_rows = lax.optimization_barrier((partial, full_rows))
        distance = 1
        while distance < row_size:
            pairs = [(i, i ^ distance) for i in range(row_size)]
            received = lax.ppermute(partial, "row", pairs)
            if distance == 2:
                received, up_query, up_value = lax.optimization_barrier(
                    (received, up_query, up_value)
                )
            partial = partial + received
            distance *= 2
        lowrank = partial.astype(jnp.bfloat16)
        onehot_b = onehot.astype(jnp.bfloat16)
        spread_query = (onehot_b[:, :, None] * lowrank[:, None, :rank_width]).reshape(
            -1, adapter_count * rank_width
        )
        spread_value = (onehot_b[:, :, None] * lowrank[:, None, rank_width:]).reshape(
            -1, adapter_count * rank_width
        )
        delta_query = jnp.dot(
            spread_query,
            up_query.reshape(adapter_count * rank_width, -1),
            preferred_element_type=jnp.float32,
        )
        delta_value = jnp.dot(
            spread_value,
            up_value.reshape(adapter_count * rank_width, -1),
            preferred_element_type=jnp.float32,
        )

    with jax.named_scope("projection"):
        base = jnp.einsum(
            "tci,cin->tn",
            full_rows.reshape(full_rows.shape[0], packed.shape[0], feature_rows),
            weights,
            preferred_element_type=jnp.float32,
        )
        base_query = base[:, :query_width]
        base_key = base[:, query_width : query_width + key_width]
        base_value = base[:, query_width + key_width :]

    with jax.named_scope("rotary"):
        half_width = HEAD // 2
        frequency = jnp.exp(
            jnp.arange(half_width, dtype=jnp.float32) * (-2.0 * math.log(10000.0) / HEAD)
        )
        angles = position.astype(jnp.float32)[:, None] * frequency[None, :]
        cosine = jnp.cos(angles)[:, None, :]
        sine_value = jnp.sin(angles)[:, None, :]
        query = rotate(base_query + delta_query, cosine, sine_value).astype(jnp.bfloat16)
        key_rotated = rotate(base_key, cosine, sine_value).astype(jnp.bfloat16)
        value_rows = (base_value + delta_value).astype(jnp.bfloat16)
        value_rows = lax.optimization_barrier(value_rows)

    with jax.named_scope("cache_write"):
        pages = page_table.shape[1]
        rows, keep = cache_rows(lengths, starts, page_table[0])
        select = (
            (rows[:, None] == jnp.arange(TOK_DEV, dtype=jnp.int32)[None, :]) & keep[:, None]
        ).astype(jnp.bfloat16)
        key_cache = jnp.dot(select, key_rotated, preferred_element_type=jnp.float32)
        key_cache = key_cache.astype(jnp.bfloat16).reshape(pages, PAGE, key_width)
        value_cache = jnp.dot(select, value_rows, preferred_element_type=jnp.float32)
        value_cache = value_cache.astype(jnp.bfloat16).reshape(pages, PAGE, key_width)
    return (query, key_cache.astype(jnp.bfloat16), value_cache.astype(jnp.bfloat16))


def solution(mesh):
    return jax.shard_map(
        shards,
        mesh=mesh,
        in_specs=(
            P("col", "row"),
            P("col", "row"),
            P("col", "row"),
            P("col", "row"),
            P("col", "row", None),
            P("col", None, "row"),
            P("col", None, "row"),
            P("col", None),
            P("col", None),
            P(),
            P("col", None),
        ),
        out_specs=(P("col", "row"), P("col", None, "row"), P("col", None, "row")),
        check_vma=False,
    )
```

```python
import math

import jax
import jax.numpy as jnp
from jax import lax
from jax.sharding import PartitionSpec as P

HEAD = 128
PAGE = 128
TOK_DEV = 1024


def rotate(values, cosine, sine_value):
    shaped = values.reshape(values.shape[0], -1, 2, HEAD // 2)
    swapped = shaped[:, :, ::-1, :]
    rotated = shaped * cosine + swapped * sine_value
    return rotated.reshape(values.shape)


def token_layout(lengths, chosen_request):
    token_index = jnp.arange(TOK_DEV, dtype=jnp.int32)
    starts = jnp.cumsum(lengths) - lengths
    inside = (token_index[:, None] >= starts[None, :]) & (
        token_index[:, None] < (starts + lengths)[None, :]
    )
    inside = inside.astype(jnp.int32)
    position = token_index - jnp.sum(inside * starts[None, :], axis=1)
    chosen = jnp.sum(inside * chosen_request[None, :], axis=1)
    return starts, position, chosen


def cache_rows(lengths, starts, page_row):
    pages = page_row.shape[0]
    pages_each = (lengths + PAGE - 1) // PAGE
    page_start = jnp.cumsum(pages_each) - pages_each
    page_ids = jnp.arange(pages, dtype=jnp.int32)
    owner = (page_row[:, None] == page_ids[None, :]).astype(jnp.int32)
    page_of_slot = jnp.sum(owner * page_ids[:, None], axis=0)
    member = (page_of_slot[:, None] >= page_start[None, :]) & (
        page_of_slot[:, None] < (page_start + pages_each)[None, :]
    )
    member = member.astype(jnp.int32)
    used = jnp.sum(member, axis=1) > 0
    first_page = jnp.sum(member * page_start[None, :], axis=1)
    first_token = jnp.sum(member * starts[None, :], axis=1)
    length = jnp.sum(member * lengths[None, :], axis=1)
    offset = (page_of_slot - first_page) * PAGE
    source = first_token + offset
    valid = jnp.where(used, jnp.minimum(length - offset, PAGE), 0)
    inner = jnp.arange(PAGE, dtype=jnp.int32)
    rows = (source[:, None] + inner[None, :]).reshape(-1)
    keep = (inner[None, :] < valid[:, None]).reshape(-1)
    rows = jnp.clip(rows, 0, TOK_DEV - 1)
    return rows, keep


def gather_rows(hidden, row_size):
    chips = row_size // 2
    assert chips == 4
    tokens, width = hidden.shape
    index = lax.axis_index("row")
    core = index % 2
    chip = index // 2
    step = 2 * core - 1
    swap = [(i, i ^ 1) for i in range(row_size)]
    ring = [
        (i, ((i // 2 + 1) % chips) * 2 if i % 2 == 0 else ((i // 2 - 1) % chips) * 2 + 1)
        for i in range(row_size)
    ]
    partner = lax.ppermute(hidden, "row", swap)
    own_block = jnp.where(
        core == 0,
        jnp.concatenate([hidden, partner], axis=1),
        jnp.concatenate([partner, hidden], axis=1),
    )
    near = lax.ppermute(own_block, "row", ring)
    half = tokens // 2
    forwarded = lax.dynamic_slice_in_dim(near, core * half, half, 0)
    far_half = lax.ppermute(forwarded, "row", ring)
    from_partner, far_other = lax.ppermute((near, far_half), "row", swap)
    first = core == 0
    after = jnp.where(first, from_partner, near)
    before = jnp.where(first, near, from_partner)
    far = jnp.where(
        first,
        jnp.concatenate([far_half, far_other], axis=0),
        jnp.concatenate([far_other, far_half], axis=0),
    )
    blocks = []
    for k in range(chips):
        relative = (k - chip) % chips
        blocks.append(
            jnp.where(
                relative == 0,
                own_block,
                jnp.where(relative == 1, after, jnp.where(relative == 2, far, before)),
            )
        )
    full = jnp.concatenate(blocks, axis=1)
    return full


def shards(
    hidden,
    w_query,
    w_key,
    w_value,
    adapter_down,
    adapter_up_query,
    adapter_up_value,
    lengths,
    request_adapter,
    adapter_slot,
    page_table,
):
    lengths = lengths[0]
    chosen_request = jnp.take(adapter_slot, request_adapter[0])
    starts, position, chosen = token_layout(lengths, chosen_request)
    adapter_count = adapter_slot.shape[0]
    rank_width = adapter_up_query.shape[1]
    query_width = w_query.shape[1]
    key_width = w_key.shape[1]

    weight_width = query_width + 2 * key_width
    feature_rows = w_query.shape[0]
    down_shape = adapter_down.shape[1:]
    row_size = lax.axis_size("row")

    with jax.named_scope("gathers"):
        full_rows = gather_rows(hidden, row_size)
        features = down_shape[0]
        spare = weight_width - features
        down_t = jnp.transpose(adapter_down[0])
        up_flat = jnp.concatenate(
            [adapter_up_query.reshape(-1), adapter_up_value.reshape(-1)]
        )
        up_flat = jnp.pad(up_flat, (0, down_t.shape[0] * spare - up_flat.shape[0]))
        down_rows = jnp.concatenate([down_t, up_flat.reshape(down_t.shape[0], spare)], axis=1)
        pieces = [
            jnp.concatenate([w_query, w_key, w_value], axis=1),
            down_rows,
        ]
        pieces = [jnp.pad(p, ((0, -p.shape[0] % 8), (0, 0))) for p in pieces]
        bounds = [0]
        for piece in pieces:
            bounds.append(bounds[-1] + piece.shape[0])
        packed = lax.all_gather(jnp.concatenate(pieces, axis=0), "col", axis=0)
        weights = packed[:, :feature_rows]
        down_local = packed[:, bounds[1] : bounds[2]].reshape(-1, weight_width)
        up_all = packed[:, bounds[1] : bounds[2], features:].reshape(adapter_count, -1)
        query_size = rank_width * query_width
        up_query = up_all[:, :query_size].reshape(adapter_count, rank_width, -1)
        up_value = up_all[:, query_size : query_size + rank_width * key_width]
        up_value = up_value.reshape(adapter_count, rank_width, -1)

    with jax.named_scope("lowrank"):
        onehot = (chosen[:, None] == jnp.arange(adapter_count, dtype=jnp.int32)[None, :])
        padded_hidden = jnp.pad(hidden, ((0, 0), (0, weight_width - features)))
        partial_all = lax.dot_general(
            padded_hidden,
            down_local,
            (((1,), (1,)), ((), ())),
            preferred_element_type=jnp.float32,
        ).reshape(hidden.shape[0], adapter_count, -1)
        partial = jnp.sum(jnp.where(onehot[:, :, None], partial_all, 0.0), axis=1)
        partial, full_rows = lax.optimization_barrier((partial, full_rows))
        distance = 1
        while distance < row_size:
            pairs = [(i, i ^ distance) for i in range(row_size)]
            received = lax.ppermute(partial, "row", pairs)
            if distance == 2:
                received, up_query, up_value = lax.optimization_barrier(
                    (received, up_query, up_value)
                )
            partial = partial + received
            distance *= 2
        lowrank = partial.astype(jnp.bfloat16)
        onehot_b = onehot.astype(jnp.bfloat16)
        spread_query = (onehot_b[:, :, None] * lowrank[:, None, :rank_width]).reshape(
            -1, adapter_count * rank_width
        )
        spread_value = (onehot_b[:, :, None] * lowrank[:, None, rank_width:]).reshape(
            -1, adapter_count * rank_width
        )
        delta_query = jnp.dot(
            spread_query,
            up_query.reshape(adapter_count * rank_width, -1),
            preferred_element_type=jnp.float32,
        )
        delta_value = jnp.dot(
            spread_value,
            up_value.reshape(adapter_count * rank_width, -1),
            preferred_element_type=jnp.float32,
        )

    with jax.named_scope("projection"):
        base = jnp.einsum(
            "tci,cin->tn",
            full_rows.reshape(full_rows.shape[0], packed.shape[0], feature_rows),
            weights,
            preferred_element_type=jnp.float32,
        )
        base_query = base[:, :query_width]
        base_key = base[:, query_width : query_width + key_width]
        base_value = base[:, query_width + key_width :]

    with jax.named_scope("rotary"):
        half_width = HEAD // 2
        frequency = jnp.exp(
            jnp.arange(half_width, dtype=jnp.float32) * (-2.0 * math.log(10000.0) / HEAD)
        )
        angles = position.astype(jnp.float32)[:, None] * frequency[None, :]
        cosine = jnp.cos(angles)[:, None, None, :]
        sine = jnp.sin(angles)
        sine_value = jnp.stack([-sine, sine], axis=1)[:, None, :, :]
        query = rotate(base_query + delta_query, cosine, sine_value).astype(jnp.bfloat16)
        key_rotated = rotate(base_key, cosine, sine_value).astype(jnp.bfloat16)
        value_rows = (base_value + delta_value).astype(jnp.bfloat16)
        value_rows = lax.optimization_barrier(value_rows)

    with jax.named_scope("cache_write"):
        pages = page_table.shape[1]
        rows, keep = cache_rows(lengths, starts, page_table[0])
        select = (
            (rows[:, None] == jnp.arange(TOK_DEV, dtype=jnp.int32)[None, :]) & keep[:, None]
        ).astype(jnp.bfloat16)
        key_cache = jnp.dot(select, key_rotated, preferred_element_type=jnp.float32)
        key_cache = key_cache.astype(jnp.bfloat16).reshape(pages, PAGE, key_width)
        value_cache = jnp.dot(select, value_rows, preferred_element_type=jnp.float32)
        value_cache = value_cache.astype(jnp.bfloat16).reshape(pages, PAGE, key_width)
    return (query, key_cache.astype(jnp.bfloat16), value_cache.astype(jnp.bfloat16))


def solution(mesh):
    return jax.shard_map(
        shards,
        mesh=mesh,
        in_specs=(
            P("col", "row"),
            P("col", "row"),
            P("col", "row"),
            P("col", "row"),
            P("col", "row", None),
            P("col", None, "row"),
            P("col", None, "row"),
            P("col", None),
            P("col", None),
            P(),
            P("col", None),
        ),
        out_specs=(P("col", "row"), P("col", None, "row"), P("col", None, "row")),
        check_vma=False,
    )
```

```python
import math

import jax
import jax.numpy as jnp
from jax import lax
from jax.sharding import PartitionSpec as P

HEAD = 128
PAGE = 128
TOK_DEV = 1024


def rotate(values, cosine, sine_value):
    half_width = HEAD // 2
    shaped = values.reshape(values.shape[0], -1, HEAD)
    leading = shaped[:, :, :half_width]
    second = shaped[:, :, half_width:]
    rotated = jnp.concatenate(
        [leading * cosine - second * sine_value, second * cosine + leading * sine_value], axis=2
    )
    return rotated.reshape(values.shape)


def token_layout(lengths, chosen_request):
    token_index = jnp.arange(TOK_DEV, dtype=jnp.int32)
    starts = jnp.cumsum(lengths) - lengths
    inside = (token_index[:, None] >= starts[None, :]) & (
        token_index[:, None] < (starts + lengths)[None, :]
    )
    inside = inside.astype(jnp.int32)
    position = token_index - jnp.sum(inside * starts[None, :], axis=1)
    chosen = jnp.sum(inside * chosen_request[None, :], axis=1)
    return starts, position, chosen


def cache_rows(lengths, starts, page_row):
    pages = page_row.shape[0]
    pages_each = (lengths + PAGE - 1) // PAGE
    page_start = jnp.cumsum(pages_each) - pages_each
    page_ids = jnp.arange(pages, dtype=jnp.int32)
    owner = (page_row[:, None] == page_ids[None, :]).astype(jnp.int32)
    page_of_slot = jnp.sum(owner * page_ids[:, None], axis=0)
    member = (page_of_slot[:, None] >= page_start[None, :]) & (
        page_of_slot[:, None] < (page_start + pages_each)[None, :]
    )
    member = member.astype(jnp.int32)
    used = jnp.sum(member, axis=1) > 0
    first_page = jnp.sum(member * page_start[None, :], axis=1)
    first_token = jnp.sum(member * starts[None, :], axis=1)
    length = jnp.sum(member * lengths[None, :], axis=1)
    offset = (page_of_slot - first_page) * PAGE
    source = first_token + offset
    valid = jnp.where(used, jnp.minimum(length - offset, PAGE), 0)
    inner = jnp.arange(PAGE, dtype=jnp.int32)
    rows = (source[:, None] + inner[None, :]).reshape(-1)
    keep = (inner[None, :] < valid[:, None]).reshape(-1)
    rows = jnp.clip(rows, 0, TOK_DEV - 1)
    return rows, keep


def gather_rows(hidden, row_size):
    chips = row_size // 2
    assert chips == 4
    tokens, width = hidden.shape
    index = lax.axis_index("row")
    core = index % 2
    chip = index // 2
    step = 2 * core - 1
    swap = [(i, i ^ 1) for i in range(row_size)]
    ring = [
        (i, ((i // 2 + 1) % chips) * 2 if i % 2 == 0 else ((i // 2 - 1) % chips) * 2 + 1)
        for i in range(row_size)
    ]
    partner = lax.ppermute(hidden, "row", swap)
    own_block = jnp.where(
        core == 0,
        jnp.concatenate([hidden, partner], axis=1),
        jnp.concatenate([partner, hidden], axis=1),
    )
    near = lax.ppermute(own_block, "row", ring)
    half = tokens // 2
    forwarded = lax.dynamic_slice_in_dim(near, core * half, half, 0)
    far_half = lax.ppermute(forwarded, "row", ring)
    from_partner, far_other = lax.ppermute((near, far_half), "row", swap)
    first = core == 0
    after = jnp.where(first, from_partner, near)
    before = jnp.where(first, near, from_partner)
    far = jnp.where(
        first,
        jnp.concatenate([far_half, far_other], axis=0),
        jnp.concatenate([far_other, far_half], axis=0),
    )
    blocks = []
    for k in range(chips):
        relative = (k - chip) % chips
        blocks.append(
            jnp.where(
                relative == 0,
                own_block,
                jnp.where(relative == 1, after, jnp.where(relative == 2, far, before)),
            )
        )
    full = jnp.concatenate(blocks, axis=1)
    return full


def shards(
    hidden,
    w_query,
    w_key,
    w_value,
    adapter_down,
    adapter_up_query,
    adapter_up_value,
    lengths,
    request_adapter,
    adapter_slot,
    page_table,
):
    lengths = lengths[0]
    chosen_request = jnp.take(adapter_slot, request_adapter[0])
    starts, position, chosen = token_layout(lengths, chosen_request)
    adapter_count = adapter_slot.shape[0]
    rank_width = adapter_up_query.shape[1]
    query_width = w_query.shape[1]
    key_width = w_key.shape[1]

    weight_width = query_width + 2 * key_width
    feature_rows = w_query.shape[0]
    down_shape = adapter_down.shape[1:]
    row_size = lax.axis_size("row")

    with jax.named_scope("gathers"):
        full_rows = gather_rows(hidden, row_size)
        features = down_shape[0]
        spare = weight_width - features
        down_t = jnp.transpose(adapter_down[0])
        up_flat = jnp.concatenate(
            [adapter_up_query.reshape(-1), adapter_up_value.reshape(-1)]
        )
        up_flat = jnp.pad(up_flat, (0, down_t.shape[0] * spare - up_flat.shape[0]))
        down_rows = jnp.concatenate([down_t, up_flat.reshape(down_t.shape[0], spare)], axis=1)
        pieces = [
            jnp.concatenate([w_query, w_key, w_value], axis=1),
            down_rows,
        ]
        pieces = [jnp.pad(p, ((0, -p.shape[0] % 8), (0, 0))) for p in pieces]
        bounds = [0]
        for piece in pieces:
            bounds.append(bounds[-1] + piece.shape[0])
        packed = lax.all_gather(jnp.concatenate(pieces, axis=0), "col", axis=0)
        weights = packed[:, :feature_rows]
        down_local = packed[:, bounds[1] : bounds[2]].reshape(-1, weight_width)
        up_all = packed[:, bounds[1] : bounds[2], features:].reshape(adapter_count, -1)
        query_size = rank_width * query_width
        up_query = up_all[:, :query_size].reshape(adapter_count, rank_width, -1)
        up_value = up_all[:, query_size : query_size + rank_width * key_width]
        up_value = up_value.reshape(adapter_count, rank_width, -1)

    with jax.named_scope("lowrank"):
        onehot = (chosen[:, None] == jnp.arange(adapter_count, dtype=jnp.int32)[None, :])
        padded_hidden = jnp.pad(hidden, ((0, 0), (0, weight_width - features)))
        partial_all = lax.dot_general(
            padded_hidden,
            down_local,
            (((1,), (1,)), ((), ())),
            preferred_element_type=jnp.float32,
        ).reshape(hidden.shape[0], adapter_count, -1)
        partial = jnp.sum(jnp.where(onehot[:, :, None], partial_all, 0.0), axis=1)
        partial, full_rows = lax.optimization_barrier((partial, full_rows))
        distance = 1
        while distance < row_size:
            pairs = [(i, i ^ distance) for i in range(row_size)]
            received = lax.ppermute(partial, "row", pairs)
            if distance == 2:
                received, up_query, up_value = lax.optimization_barrier(
                    (received, up_query, up_value)
                )
            partial = partial + received
            distance *= 2
        lowrank = partial.astype(jnp.bfloat16)
        onehot_b = onehot.astype(jnp.bfloat16)
        spread_query = (onehot_b[:, :, None] * lowrank[:, None, :rank_width]).reshape(
            -1, adapter_count * rank_width
        )
        spread_value = (onehot_b[:, :, None] * lowrank[:, None, rank_width:]).reshape(
            -1, adapter_count * rank_width
        )
        delta_query = jnp.dot(
            spread_query,
            up_query.reshape(adapter_count * rank_width, -1),
            preferred_element_type=jnp.float32,
        )
        delta_value = jnp.dot(
            spread_value,
            up_value.reshape(adapter_count * rank_width, -1),
            preferred_element_type=jnp.float32,
        )

    with jax.named_scope("projection"):
        base = jnp.einsum(
            "tci,cin->tn",
            full_rows.reshape(full_rows.shape[0], packed.shape[0], feature_rows),
            weights,
            preferred_element_type=jnp.float32,
        )
        base_query = base[:, :query_width]
        base_key = base[:, query_width : query_width + key_width]
        base_value = base[:, query_width + key_width :]

    with jax.named_scope("rotary"):
        half_width = HEAD // 2
        frequency = jnp.exp(
            jnp.arange(half_width, dtype=jnp.float32) * (-2.0 * math.log(10000.0) / HEAD)
        )
        angles = position.astype(jnp.float32)[:, None] * frequency[None, :]
        cosine = jnp.cos(angles)[:, None, :]
        sine_value = jnp.sin(angles)[:, None, :]
        query = rotate(base_query + delta_query, cosine, sine_value).astype(jnp.bfloat16)
        key_rotated = rotate(base_key, cosine, sine_value).astype(jnp.bfloat16)
        key_rotated = lax.optimization_barrier(key_rotated)
        value_rows = (base_value + delta_value).astype(jnp.bfloat16)
        value_rows = lax.optimization_barrier(value_rows)

    with jax.named_scope("cache_write"):
        pages = page_table.shape[1]
        rows, keep = cache_rows(lengths, starts, page_table[0])
        select = (
            (rows[:, None] == jnp.arange(TOK_DEV, dtype=jnp.int32)[None, :]) & keep[:, None]
        ).astype(jnp.bfloat16)
        key_cache = jnp.dot(select, key_rotated, preferred_element_type=jnp.float32)
        key_cache = key_cache.astype(jnp.bfloat16).reshape(pages, PAGE, key_width)
        value_cache = jnp.dot(select, value_rows, preferred_element_type=jnp.float32)
        value_cache = value_cache.astype(jnp.bfloat16).reshape(pages, PAGE, key_width)
    return (query, key_cache.astype(jnp.bfloat16), value_cache.astype(jnp.bfloat16))


def solution(mesh):
    return jax.shard_map(
        shards,
        mesh=mesh,
        in_specs=(
            P("col", "row"),
            P("col", "row"),
            P("col", "row"),
            P("col", "row"),
            P("col", "row", None),
            P("col", None, "row"),
            P("col", None, "row"),
            P("col", None),
            P("col", None),
            P(),
            P("col", None),
        ),
        out_specs=(P("col", "row"), P("col", None, "row"), P("col", None, "row")),
        check_vma=False,
    )
```
